128 devices in a mesh: mass: 4 (over y), shard: 32 (over x, z, core).
Axes of the slice: x: 4, y: 4, z: 4, core: 2. Of those that a mesh axis runs over, the one named last changes fastest.
Arguments:
- queries: bfloat16 [2048, 8192], P(('mass', 'shard')), may hold values from -6 to 6
- library: bfloat16 [131072, 8192], P(('mass', 'shard')), may hold values from -0.0625 to 0.0625
- routes: int32 [2048, 1], P(('mass', 'shard')), may hold values from 0 to 3; in each aligned block of 16 rows (0 to 15, 16 to 31, ...) at most 8 rows name the same one
- offsets: int32 [2048], P(('mass', 'shard')), may hold values from -2048 to 2048
Outputs:
- best_scores: float32 [2048, 16], P(('mass', 'shard'))
The draws below stay inside these ranges and needn't reach their ends.
Inputs may be any that keep to these rules, and one draw needn't show every extreme that they name: `routes`: in each device's aligned block of 16 queries at most 8 go to one mass group, and some group gets exactly 8 from some device.
All inputs are finite; a program needn't handle non-finite values.
Results may differ from the reference program's by a relative error of at most 0.00087.
Values may be sent and summed in bfloat16 or wider, within the bound.
No kernel may reach another device: no remote copies, remote signals or barrier semaphores. Data moves between devices by JAX's collectives and lax.ppermute only.
A program may use at most 128 MiB of HBM per device.

```python
import math
import jax
import jax.numpy as jnp
import numpy as np
from jax import lax

BINS = 8192
MAX_SHIFT = 2048
TOP_K = 16
LIB_DEV = 1024
Q_DEV = 16
CAP = 8
Q_TOTAL = 2048
LIB = 131072
N_MASS = 4
N_SHARD = 32
DEVICES = 128


def touch_ends(result, stream_key, smallest, top_value):
    index_at = [jax.random.randint(jax.random.fold_in(stream_key, axis), (), 0, length) for axis, length in enumerate(result.shape)]
    widest = result.shape.index(max(result.shape))
    beside = index_at[:widest] + [(index_at[widest] + 1) % result.shape[widest]] + index_at[widest + 1:]
    return result.at[tuple(index_at)].set(smallest).at[tuple(beside)].set(top_value)


def shard_levels(rng, extent, split, least, largest):
    factor_of, own = 1.0, jax.random.fold_in(rng, 6)
    for position, blocks in split:
        steps = jnp.exp(jax.random.uniform(jax.random.fold_in(own, position), (blocks,), jnp.float32, least / len(split), largest / len(split)))
        factor_of = factor_of * jnp.repeat(steps, extent[position] // blocks).reshape([-1 if axis == position else 1 for axis in range(len(extent))])
    return factor_of


def shared_out(rng, own, number, rows, count, top, bound, lean):
    order = jax.random.permutation(rng, count)
    crowded, common = shares(count, rows * top, bound, lean, True), shares(count, rows * top, bound, lean, False)
    places = jnp.arange(count)

    def named(sizes, rotation):
        used = int((sizes > 0).sum())
        fixed = max(1, used // 4)
        moved = fixed + (places - fixed + rotation * (used - fixed)) % max(1, count - fixed)
        return jnp.zeros((count,), jnp.int32).at[order[jnp.where(places < fixed, places, moved)]].set(jnp.asarray(sizes, jnp.int32))

    sizes = jnp.where(number % 4 == 0, named(crowded, number // 4), named(common, number - number // 4 - 1))
    mixed = jax.random.permutation(jax.random.fold_in(own, 3), count)
    giver, taker = mixed[0:count // 2 * 2:2], mixed[1:count // 2 * 2:2]
    margin = jnp.minimum(sizes[giver] - 1, bound - sizes[taker]) // 2
    margin = jnp.where((giver == order[0]) | (taker == order[0]) | (sizes[taker] == 0), 0, jnp.maximum(margin, 0))
    moved = jax.random.randint(jax.random.fold_in(own, 4), (count // 2,), 0, 1 << 20) % (margin + 1)
    sizes = sizes.at[giver].add(-moved).at[taker].add(moved)
    labels = jnp.searchsorted(jnp.cumsum(sizes), jnp.arange(rows * top), side="right").astype(jnp.int32)
    listing = labels.reshape(top, rows).T
    listing = listing[jax.random.permutation(jax.random.fold_in(own, 1), rows)]
    rotation = jax.random.randint(jax.random.fold_in(own, 2), (rows, 1), 0, top)
    return jnp.take_along_axis(listing, (jnp.arange(top)[None, :] + rotation) % top, axis=1)


def shares(number_of, total, reach, skew, full):
    weights = [(1 << 20) // math.isqrt(standing ** skew) + 1 for standing in range(1, number_of + 1)]
    largest = reach if full else min(reach, max(-(-total // number_of), total * weights[0] // sum(weights)))
    least = 1 if total - largest >= number_of - 1 else 0
    counts, spare = [largest] + [least] * (number_of - 1), total - largest - least * (number_of - 1)
    while spare > 0:
        movable = [i for i in range(1, number_of) if counts[i] < largest] or [i for i in range(1, number_of) if counts[i] < reach]
        mass, remaining = sum([weights[i] for i in movable]), spare
        for i in movable:
            extra = min(reach - counts[i], max(1, remaining * weights[i] // mass), spare)
            counts[i] = counts[i] + extra
            spare = spare - extra
    return np.array(counts)


def centred(rng, dims, spread, bound, shards=(), kind=jnp.bfloat16):
    entries = spread * jax.random.normal(rng, dims, jnp.float32)
    if shards:
        entries = entries * shard_levels(rng, dims, shards, -0.22, 0.18)
    return jnp.clip(entries, -bound, bound).astype(kind)


def setup_inputs(seed: int = 0) -> dict:
    keys = jax.random.split(jax.random.key(seed), 5)
    queries = centred(keys[0], (Q_TOTAL, BINS), 1.0, 6.0, ((0, 128),))
    library = centred(keys[1], (LIB, BINS), BINS ** -0.5, 0.0625, ((0, 128),))
    routes_keys = jax.random.split(jax.random.fold_in(keys[2], 1), Q_TOTAL // Q_DEV)
    routes_turns = jax.random.permutation(jax.random.fold_in(keys[2], 3), Q_TOTAL // Q_DEV)
    routes = jax.vmap(lambda own, number: shared_out(jax.random.fold_in(keys[2], 2), own, number, Q_DEV, N_MASS, 1, CAP, 2))(routes_keys, routes_turns).reshape((Q_TOTAL, 1))
    offsets = touch_ends(jax.random.randint(keys[3], (Q_TOTAL,), -MAX_SHIFT, MAX_SHIFT + 1), jax.random.fold_in(keys[3], 1), -MAX_SHIFT, MAX_SHIFT).astype(jnp.int32)
    return dict(queries=queries, library=library, routes=routes, offsets=offsets)


def shifted_spectra(queries, offsets):
    bin_count = queries.shape[1]
    positions = jnp.arange(bin_count, dtype=jnp.int32)
    source_bin = positions[None, :] - offsets[:, None].astype(jnp.int32)
    inside = (source_bin >= 0) & (source_bin < bin_count)
    shifted = jnp.take_along_axis(queries, jnp.clip(source_bin, 0, bin_count - 1), axis=1)
    combined = queries.astype(jnp.float32) + jnp.where(inside, shifted.astype(jnp.float32), jnp.float32(0.0))
    scale_factor = lax.rsqrt(lax.optimization_barrier(jnp.mean(combined * combined, axis=1, keepdims=True)) + 1e-06)
    return (combined * scale_factor).astype(jnp.bfloat16)

def block_ranks(dest_group):
    length = dest_group.shape[0]
    position_ids = jnp.arange(length, dtype=jnp.int32)
    earlier = (dest_group[:, None] == dest_group[None, :]) & (position_ids[:, None] > position_ids[None, :])
    return lax.optimization_barrier(jnp.sum(earlier.astype(jnp.int32), axis=1)).astype(jnp.int32)

def reference(queries, library, routes, offsets):
    spectra = shifted_spectra(queries, offsets)
    dest_group = routes[:, 0].astype(jnp.int32)
    ranks_all = jax.vmap(block_ranks)(dest_group.reshape(DEVICES, Q_DEV)).reshape(-1)
    query_ids = jnp.arange(DEVICES * Q_DEV, dtype=jnp.int32)
    slot_index = query_ids // Q_DEV * CAP + ranks_all
    slot_total = DEVICES * CAP
    grouped_library = library.reshape(N_MASS, N_SHARD * LIB_DEV, BINS)

    def per_group(operands):
        library_group, group_id = operands
        target = jnp.where(dest_group == group_id, slot_index, slot_total).astype(jnp.int32)
        picker = jnp.zeros((slot_total + 1,), jnp.int32).at[target].set(query_ids)
        filled = jnp.zeros((slot_total + 1,), jnp.int32).at[target].set(1)
        picked = jnp.take(spectra, picker[:slot_total], axis=0)
        picked = jnp.where(filled[:slot_total, None] == 1, picked, jnp.zeros_like(picked))
        scores = lax.dot_general(picked, library_group, (((1,), (1,)), ((), ())), preferred_element_type=jnp.float32)
        return lax.top_k(scores, TOP_K)[0]
    results = lax.map(per_group, (grouped_library, jnp.arange(N_MASS, dtype=jnp.int32)))
    return results[dest_group, slot_index]
```

```python
import functools

import jax
import jax.numpy as jnp
from jax import lax
from jax.experimental import pallas as pl
from jax.experimental.pallas import tpu as pltpu
from jax.sharding import Mesh
from jax.sharding import PartitionSpec as P

MAX_SHIFT = 2048
TOP_K = 16
LANES = 128
SUBLANES = 8


def shifted_spectra(queries, offsets):
    row_count = queries.shape[0]
    bin_count = queries.shape[1]
    margin = jnp.zeros((row_count, MAX_SHIFT), queries.dtype)
    current = jnp.concatenate([margin, queries, margin], axis=1)
    window_start = MAX_SHIFT - offsets
    bit_total = (2 * MAX_SHIFT).bit_length()
    for bit_number in range(bit_total):
        step_size = 1 << bit_number
        moved = jnp.concatenate(
            [current[:, step_size:], jnp.zeros((row_count, step_size), current.dtype)], axis=1
        )
        taken = window_start >> bit_number & 1 == 1
        current = jnp.where(taken[:, None], moved, current)
    shifted = current[:, :bin_count]
    combined = queries.astype(jnp.float32) + shifted.astype(jnp.float32)
    scale_factor = lax.rsqrt(jnp.mean(combined * combined, axis=1, keepdims=True) + 1e-06)
    return (combined * scale_factor).astype(jnp.bfloat16)


def block_ranks(dest_group):
    length = dest_group.shape[0]
    position_ids = jnp.arange(length, dtype=jnp.int32)
    earlier = (dest_group[:, None] == dest_group[None, :]) & (
        position_ids[:, None] > position_ids[None, :]
    )
    return jnp.sum(earlier.astype(jnp.int32), axis=1)


def merge_sorted(first, second):
    merged = [jnp.maximum(first[k], second[TOP_K - 1 - k]) for k in range(TOP_K)]
    span = TOP_K // 2
    while span >= 1:
        for k in range(TOP_K):
            if (k // span) % 2 == 0:
                upper, lower = merged[k], merged[k + span]
                merged[k] = jnp.maximum(upper, lower)
                merged[k + span] = jnp.minimum(upper, lower)
        span //= 2
    return merged


def column_topk_kernel(scores_ref, out_ref):
    steps = scores_ref.shape[0] // SUBLANES
    lowest = jnp.full((SUBLANES, LANES), -jnp.inf, jnp.float32)

    def insert(step, kept):
        start = pl.multiple_of(step * SUBLANES, SUBLANES)
        value = scores_ref[pl.ds(start, SUBLANES), :]
        updated = []
        for k in range(TOP_K):
            updated.append(jnp.maximum(kept[k], value))
            value = jnp.minimum(kept[k], value)
        return tuple(updated)

    kept = lax.fori_loop(0, steps, insert, (lowest,) * TOP_K, unroll=8)
    kept = list(kept)
    shift = SUBLANES // 2
    while shift >= 1:
        rolled = [pltpu.roll(kept[k], shift, 0) for k in range(TOP_K)]
        kept = merge_sorted(kept, rolled)
        shift //= 2
    for k in range(TOP_K):
        out_ref[pl.ds(k, 1), :] = kept[k][0:1, :]


def column_topk(scores):
    rows, columns = scores.shape
    return pl.pallas_call(
        column_topk_kernel,
        out_shape=jax.ShapeDtypeStruct((TOP_K, columns), jnp.float32),
        grid=(columns // LANES,),
        in_specs=[pl.BlockSpec((rows, LANES), lambda j: (0, j))],
        out_specs=pl.BlockSpec((TOP_K, LANES), lambda j: (0, j)),
        cost_estimate=pl.CostEstimate(
            flops=2 * TOP_K * rows * columns, transcendentals=0, bytes_accessed=4 * rows * columns
        ),
    )(scores)


def per_device(queries, library, routes, offsets):
    mass_count = lax.axis_size("mass")
    shard_count = lax.axis_size("shard")
    query_count = queries.shape[0]
    capacity = query_count // 2
    spectra = shifted_spectra(queries, offsets)
    dest_group = routes[:, 0]
    slot_index = dest_group * capacity + block_ranks(dest_group)
    selector = (
        jnp.arange(mass_count * capacity, dtype=jnp.int32)[:, None] == slot_index[None, :]
    ).astype(jnp.bfloat16)
    packed = jnp.dot(selector, spectra, preferred_element_type=jnp.float32).astype(jnp.bfloat16)
    arrived = lax.all_to_all(packed, "mass", split_axis=0, concat_axis=0, tiled=True)
    gathered = lax.all_gather(arrived, "shard", axis=0, tiled=True)
    scores_t = lax.dot_general(
        library, gathered, (((1,), (1,)), ((), ())), preferred_element_type=jnp.float32
    )
    local_best = column_topk(scores_t)
    slots_per_shard = mass_count * capacity
    outgoing = local_best.T.reshape(shard_count, slots_per_shard, TOP_K)
    incoming = lax.all_to_all(outgoing, "shard", split_axis=0, concat_axis=0, tiled=True)
    candidates = incoming.transpose(1, 0, 2).reshape(slots_per_shard, shard_count * TOP_K)
    own_best = lax.top_k(candidates, TOP_K)[0]
    returned_best = lax.all_to_all(own_best, "mass", split_axis=0, concat_axis=0, tiled=True)
    slot_match = slot_index[:, None] == jnp.arange(mass_count * capacity, dtype=jnp.int32)[None, :]
    return jnp.sum(
        jnp.where(slot_match[:, :, None], returned_best[None, :, :], jnp.float32(0.0)), axis=1
    )


def solution(mesh):
    placed = (
        P(("mass", "shard"), None),
        P(("mass", "shard"), None),
        P(("mass", "shard"), None),
        P(("mass", "shard")),
    )
    return jax.shard_map(
        per_device,
        mesh=mesh,
        in_specs=placed,
        out_specs=P(("mass", "shard"), None),
        check_vma=False,
    )
```

```python
import functools

import jax
import jax.numpy as jnp
from jax import lax
from jax.experimental import pallas as pl
from jax.experimental.pallas import tpu as pltpu
from jax.sharding import Mesh
from jax.sharding import PartitionSpec as P

MAX_SHIFT = 2048
TOP_K = 16
LANES = 128
SUBLANES = 8


def shifted_spectra(queries, offsets):
    row_count = queries.shape[0]
    bin_count = queries.shape[1]
    margin = jnp.zeros((row_count, MAX_SHIFT), queries.dtype)
    current = jnp.concatenate([margin, queries, margin], axis=1)
    window_start = MAX_SHIFT - offsets
    bit_total = (2 * MAX_SHIFT).bit_length()
    for bit_number in range(bit_total):
        step_size = 1 << bit_number
        moved = jnp.concatenate(
            [current[:, step_size:], jnp.zeros((row_count, step_size), current.dtype)], axis=1
        )
        taken = window_start >> bit_number & 1 == 1
        current = jnp.where(taken[:, None], moved, current)
    shifted = current[:, :bin_count]
    combined = queries.astype(jnp.float32) + shifted.astype(jnp.float32)
    scale_factor = lax.rsqrt(jnp.mean(combined * combined, axis=1, keepdims=True) + 1e-06)
    return (combined * scale_factor).astype(jnp.bfloat16)


def block_ranks(dest_group):
    length = dest_group.shape[0]
    position_ids = jnp.arange(length, dtype=jnp.int32)
    earlier = (dest_group[:, None] == dest_group[None, :]) & (
        position_ids[:, None] > position_ids[None, :]
    )
    return jnp.sum(earlier.astype(jnp.int32), axis=1)


def merge_sorted(first, second):
    merged = [jnp.maximum(first[k], second[TOP_K - 1 - k]) for k in range(TOP_K)]
    span = TOP_K // 2
    while span >= 1:
        for k in range(TOP_K):
            if (k // span) % 2 == 0:
                upper, lower = merged[k], merged[k + span]
                merged[k] = jnp.maximum(upper, lower)
                merged[k + span] = jnp.minimum(upper, lower)
        span //= 2
    return merged


def column_topk_kernel(scores_ref, out_ref):
    steps = scores_ref.shape[0] // SUBLANES
    lowest = jnp.full((SUBLANES, LANES), -jnp.inf, jnp.float32)

    def insert(step, kept):
        start = pl.multiple_of(step * SUBLANES, SUBLANES)
        value = scores_ref[pl.ds(start, SUBLANES), :]
        updated = []
        for k in range(TOP_K):
            updated.append(jnp.maximum(kept[k], value))
            value = jnp.minimum(kept[k], value)
        return tuple(updated)

    kept = lax.fori_loop(0, steps, insert, (lowest,) * TOP_K, unroll=8)
    kept = list(kept)
    shift = SUBLANES // 2
    while shift >= 1:
        rolled = [pltpu.roll(kept[k], shift, 0) for k in range(TOP_K)]
        kept = merge_sorted(kept, rolled)
        shift //= 2
    for k in range(TOP_K):
        out_ref[pl.ds(k, 1), :] = kept[k][0:1, :]


def column_topk(scores):
    rows, columns = scores.shape
    return pl.pallas_call(
        column_topk_kernel,
        out_shape=jax.ShapeDtypeStruct((TOP_K, columns), jnp.float32),
        grid=(columns // LANES,),
        in_specs=[pl.BlockSpec((rows, LANES), lambda j: (0, j))],
        out_specs=pl.BlockSpec((TOP_K, LANES), lambda j: (0, j)),
        cost_estimate=pl.CostEstimate(
            flops=2 * TOP_K * rows * columns, transcendentals=0, bytes_accessed=4 * rows * columns
        ),
    )(scores)


def take_group(packed, group):
    chooser = (jnp.arange(packed.shape[0], dtype=jnp.int32) == group).astype(packed.dtype)
    return jnp.einsum("g,gsb->sb", chooser, packed)


def per_device(queries, library, routes, offsets):
    mass_count = lax.axis_size("mass")
    core_count = lax.axis_size("core")
    query_count = queries.shape[0]
    capacity = query_count // 2
    own_mass = lax.axis_index("mass")
    own_core = lax.axis_index("core")
    spectra = shifted_spectra(queries, offsets)
    dest_group = routes[:, 0]
    ranks = block_ranks(dest_group)
    slot_index = dest_group * capacity + ranks
    selector = (
        jnp.arange(mass_count * capacity, dtype=jnp.int32)[:, None] == slot_index[None, :]
    ).astype(jnp.bfloat16)
    packed = jnp.dot(selector, spectra, preferred_element_type=jnp.float32).astype(jnp.bfloat16)
    packed = packed.reshape(mass_count, capacity, packed.shape[-1])
    partner = [(core, core_count - 1 - core) for core in range(core_count)]
    chunk_best = []
    for distance in range(mass_count):
        outgoing = take_group(packed, (own_mass + distance) % mass_count)
        if distance == 0:
            incoming = outgoing
        else:
            incoming = lax.ppermute(
                outgoing,
                "mass",
                [(source, (source + distance) % mass_count) for source in range(mass_count)],
            )
        own_side = lax.all_gather(incoming, "xz", axis=0, tiled=True)
        other_side = lax.ppermute(own_side, "core", partner)
        both = jnp.concatenate([own_side, other_side], axis=0)
        scores_t = lax.dot_general(
            library, both, (((1,), (1,)), ((), ())), preferred_element_type=jnp.float32
        )
        chunk_best.append(column_topk(scores_t))
    xz_count = lax.axis_size("xz")
    stacked = jnp.stack(chunk_best).reshape(mass_count, TOP_K, core_count, xz_count, capacity)
    stacked = stacked.transpose(0, 2, 3, 4, 1)
    source_mass = jnp.arange(mass_count, dtype=jnp.int32)
    by_mass = jnp.take(stacked, (own_mass - source_mass) % mass_count, axis=0)
    side_of_core = jnp.where(jnp.arange(core_count, dtype=jnp.int32) == own_core, 0, 1)
    by_core = jnp.take(by_mass, side_of_core, axis=1)
    outgoing = by_core.transpose(0, 2, 1, 3, 4).reshape(-1, capacity, TOP_K)
    received = lax.all_to_all(
        outgoing, ("mass", "xz", "core"), split_axis=0, concat_axis=0, tiled=True
    )
    received = received.reshape(mass_count, xz_count * core_count, capacity, TOP_K)
    received = received.transpose(0, 2, 1, 3).reshape(mass_count * capacity, -1)
    candidates = jnp.take(received, slot_index, axis=0)
    return lax.top_k(candidates, TOP_K)[0]


def solution(mesh):
    mass_count, shard_count = mesh.devices.shape
    core_count = 2
    split_mesh = Mesh(
        mesh.devices.reshape(mass_count, shard_count // core_count, core_count),
        ("mass", "xz", "core"),
    )
    spread = ("mass", "xz", "core")
    placed = (P(spread, None), P(spread, None), P(spread, None), P(spread))
    return jax.shard_map(
        per_device,
        mesh=split_mesh,
        in_specs=placed,
        out_specs=P(spread, None),
        check_vma=False,
    )
```

```python
import functools

import jax
import jax.numpy as jnp
from jax import lax
from jax.experimental import pallas as pl
from jax.experimental.pallas import tpu as pltpu
from jax.sharding import Mesh
from jax.sharding import PartitionSpec as P

MAX_SHIFT = 2048
TOP_K = 16
LANES = 128
SUBLANES = 8


def shifted_spectra(queries, offsets):
    row_count = queries.shape[0]
    bin_count = queries.shape[1]
    margin = jnp.zeros((row_count, MAX_SHIFT), queries.dtype)
    current = jnp.concatenate([margin, queries, margin], axis=1)
    window_start = MAX_SHIFT - offsets
    bit_total = (2 * MAX_SHIFT).bit_length()
    for bit_number in range(bit_total):
        step_size = 1 << bit_number
        moved = jnp.concatenate(
            [current[:, step_size:], jnp.zeros((row_count, step_size), current.dtype)], axis=1
        )
        taken = window_start >> bit_number & 1 == 1
        current = jnp.where(taken[:, None], moved, current)
    shifted = current[:, :bin_count]
    combined = queries.astype(jnp.float32) + shifted.astype(jnp.float32)
    scale_factor = lax.rsqrt(jnp.mean(combined * combined, axis=1, keepdims=True) + 1e-06)
    return (combined * scale_factor).astype(jnp.bfloat16)


def block_ranks(dest_group):
    length = dest_group.shape[0]
    position_ids = jnp.arange(length, dtype=jnp.int32)
    earlier = (dest_group[:, None] == dest_group[None, :]) & (
        position_ids[:, None] > position_ids[None, :]
    )
    return jnp.sum(earlier.astype(jnp.int32), axis=1)


def merge_sorted(first, second):
    merged = [jnp.maximum(first[k], second[TOP_K - 1 - k]) for k in range(TOP_K)]
    span = TOP_K // 2
    while span >= 1:
        for k in range(TOP_K):
            if (k // span) % 2 == 0:
                upper, lower = merged[k], merged[k + span]
                merged[k] = jnp.maximum(upper, lower)
                merged[k + span] = jnp.minimum(upper, lower)
        span //= 2
    return merged


def column_topk_kernel(scores_ref, out_ref):
    steps = scores_ref.shape[0] // SUBLANES
    lowest = jnp.full((SUBLANES, LANES), -jnp.inf, jnp.float32)

    def insert(step, kept):
        start = pl.multiple_of(step * SUBLANES, SUBLANES)
        value = scores_ref[pl.ds(start, SUBLANES), :]
        updated = []
        for k in range(TOP_K):
            updated.append(jnp.maximum(kept[k], value))
            value = jnp.minimum(kept[k], value)
        return tuple(updated)

    kept = lax.fori_loop(0, steps, insert, (lowest,) * TOP_K, unroll=8)
    kept = list(kept)
    shift = SUBLANES // 2
    while shift >= 1:
        rolled = [pltpu.roll(kept[k], shift, 0) for k in range(TOP_K)]
        kept = merge_sorted(kept, rolled)
        shift //= 2
    for k in range(TOP_K):
        out_ref[pl.ds(k, 1), :] = kept[k][0:1, :]


def column_topk(scores):
    rows, columns = scores.shape
    return pl.pallas_call(
        column_topk_kernel,
        out_shape=jax.ShapeDtypeStruct((TOP_K, columns), jnp.float32),
        grid=(columns // LANES,),
        in_specs=[pl.BlockSpec((rows, LANES), lambda j: (0, j))],
        out_specs=pl.BlockSpec((TOP_K, LANES), lambda j: (0, j)),
        cost_estimate=pl.CostEstimate(
            flops=2 * TOP_K * rows * columns, transcendentals=0, bytes_accessed=4 * rows * columns
        ),
    )(scores)


def per_device(queries, library, routes, offsets):
    mass_count = lax.axis_size("mass")
    shard_count = lax.axis_size("xz") * lax.axis_size("core")
    query_count = queries.shape[0]
    capacity = query_count // 2
    spectra = shifted_spectra(queries, offsets)
    dest_group = routes[:, 0]
    slot_index = dest_group * capacity + block_ranks(dest_group)
    selector = (
        jnp.arange(mass_count * capacity, dtype=jnp.int32)[:, None] == slot_index[None, :]
    ).astype(jnp.bfloat16)
    packed = jnp.dot(selector, spectra, preferred_element_type=jnp.float32).astype(jnp.bfloat16)
    arrived = lax.all_to_all(packed, "mass", split_axis=0, concat_axis=0, tiled=True)
    gathered = lax.all_gather(arrived, ("xz", "core"), axis=0, tiled=True)
    scores_t = lax.dot_general(
        library, gathered, (((1,), (1,)), ((), ())), preferred_element_type=jnp.float32
    )
    local_best = column_topk(scores_t)
    outgoing = local_best.T.reshape(shard_count, mass_count, capacity, TOP_K)
    outgoing = outgoing.transpose(1, 0, 2, 3).reshape(-1, capacity, TOP_K)
    received = lax.all_to_all(
        outgoing, ("mass", "xz", "core"), split_axis=0, concat_axis=0, tiled=True
    )
    received = received.reshape(mass_count, shard_count, capacity, TOP_K)
    received = received.transpose(0, 2, 1, 3).reshape(mass_count * capacity, -1)
    candidates = jnp.take(received, slot_index, axis=0)
    return lax.top_k(candidates, TOP_K)[0]


def solution(mesh):
    mass_count, shard_count = mesh.devices.shape
    core_count = 2
    split_mesh = Mesh(
        mesh.devices.reshape(mass_count, shard_count // core_count, core_count),
        ("mass", "xz", "core"),
    )
    spread = ("mass", "xz", "core")
    placed = (P(spread, None), P(spread, None), P(spread, None), P(spread))
    return jax.shard_map(
        per_device,
        mesh=split_mesh,
        in_specs=placed,
        out_specs=P(spread, None),
        check_vma=False,
    )
```

```python
import functools

import jax
import jax.numpy as jnp
from jax import lax
from jax.experimental import pallas as pl
from jax.experimental.pallas import tpu as pltpu
from jax.sharding import Mesh
from jax.sharding import PartitionSpec as P

MAX_SHIFT = 2048
TOP_K = 16
LANES = 128
SUBLANES = 8


def shifted_spectra(queries, offsets):
    row_count = queries.shape[0]
    bin_count = queries.shape[1]
    margin = jnp.zeros((row_count, MAX_SHIFT), queries.dtype)
    current = jnp.concatenate([margin, queries, margin], axis=1)
    window_start = MAX_SHIFT - offsets
    bit_total = (2 * MAX_SHIFT).bit_length()
    for bit_number in range(bit_total):
        step_size = 1 << bit_number
        moved = jnp.concatenate(
            [current[:, step_size:], jnp.zeros((row_count, step_size), current.dtype)], axis=1
        )
        taken = window_start >> bit_number & 1 == 1
        current = jnp.where(taken[:, None], moved, current)
    shifted = current[:, :bin_count]
    combined = queries.astype(jnp.float32) + shifted.astype(jnp.float32)
    scale_factor = lax.rsqrt(jnp.mean(combined * combined, axis=1, keepdims=True) + 1e-06)
    return (combined * scale_factor).astype(jnp.bfloat16)


def block_ranks(dest_group):
    length = dest_group.shape[0]
    position_ids = jnp.arange(length, dtype=jnp.int32)
    earlier = (dest_group[:, None] == dest_group[None, :]) & (
        position_ids[:, None] > position_ids[None, :]
    )
    return jnp.sum(earlier.astype(jnp.int32), axis=1)


def merge_sorted(first, second):
    merged = [jnp.maximum(first[k], second[TOP_K - 1 - k]) for k in range(TOP_K)]
    span = TOP_K // 2
    while span >= 1:
        for k in range(TOP_K):
            if (k // span) % 2 == 0:
                upper, lower = merged[k], merged[k + span]
                merged[k] = jnp.maximum(upper, lower)
                merged[k + span] = jnp.minimum(upper, lower)
        span //= 2
    return merged


def column_topk_kernel(scores_ref, out_ref):
    steps = scores_ref.shape[0] // SUBLANES
    lowest = jnp.full((SUBLANES, LANES), -jnp.inf, jnp.float32)

    def insert(step, kept):
        start = pl.multiple_of(step * SUBLANES, SUBLANES)
        value = scores_ref[pl.ds(start, SUBLANES), :]
        updated = []
        for k in range(TOP_K):
            updated.append(jnp.maximum(kept[k], value))
            value = jnp.minimum(kept[k], value)
        return tuple(updated)

    kept = lax.fori_loop(0, steps, insert, (lowest,) * TOP_K, unroll=8)
    kept = list(kept)
    shift = SUBLANES // 2
    while shift >= 1:
        rolled = [pltpu.roll(kept[k], shift, 0) for k in range(TOP_K)]
        kept = merge_sorted(kept, rolled)
        shift //= 2
    for k in range(TOP_K):
        out_ref[pl.ds(k, 1), :] = kept[k][0:1, :]


def column_topk(scores):
    rows, columns = scores.shape
    return pl.pallas_call(
        column_topk_kernel,
        out_shape=jax.ShapeDtypeStruct((TOP_K, columns), jnp.float32),
        grid=(columns // LANES,),
        in_specs=[pl.BlockSpec((rows, LANES), lambda j: (0, j))],
        out_specs=pl.BlockSpec((TOP_K, LANES), lambda j: (0, j)),
        cost_estimate=pl.CostEstimate(
            flops=2 * TOP_K * rows * columns, transcendentals=0, bytes_accessed=4 * rows * columns
        ),
    )(scores)


def ring_gather(block, axis):
    size = 4
    flat = block.reshape(-1, block.shape[-1])
    half = flat.shape[0] // 2
    forward = [(i, (i + 1) % size) for i in range(size)]
    backward = [(i, (i - 1) % size) for i in range(size)]
    from_minus = lax.ppermute(flat, axis, forward)
    from_plus = lax.ppermute(flat, axis, backward)
    far_first = lax.ppermute(from_minus[:half], axis, forward)
    far_second = lax.ppermute(from_plus[half:], axis, backward)
    far = jnp.concatenate([far_first, far_second], axis=0)
    stacked = jnp.stack([flat, from_plus, far, from_minus])
    return stacked.reshape((size,) + block.shape)


def per_device(queries, library, routes, offsets):
    mass_count = lax.axis_size("mass")
    x_count = lax.axis_size("x")
    z_count = lax.axis_size("z")
    core_count = lax.axis_size("core")
    shard_count = x_count * z_count * core_count
    query_count = queries.shape[0]
    capacity = query_count // 2
    spectra = shifted_spectra(queries, offsets)
    dest_group = routes[:, 0]
    slot_index = dest_group * capacity + block_ranks(dest_group)
    selector = (
        jnp.arange(mass_count * capacity, dtype=jnp.int32)[:, None] == slot_index[None, :]
    ).astype(jnp.bfloat16)
    packed = jnp.dot(selector, spectra, preferred_element_type=jnp.float32).astype(jnp.bfloat16)
    arrived = lax.all_to_all(packed, "mass", split_axis=0, concat_axis=0, tiled=True)
    part = arrived.shape[0] // 2
    part_a = ring_gather(ring_gather(arrived[:part], "x"), "z")
    part_b = ring_gather(ring_gather(arrived[part:], "z"), "x")
    own_side = jnp.concatenate(
        [part_a.reshape(-1, arrived.shape[1]), part_b.reshape(-1, arrived.shape[1])], axis=0
    )
    partner = [(core, core_count - 1 - core) for core in range(core_count)]
    other_side = lax.ppermute(own_side, "core", partner)
    own_best = column_topk(
        lax.dot_general(
            library, own_side, (((1,), (1,)), ((), ())), preferred_element_type=jnp.float32
        )
    )
    other_best = column_topk(
        lax.dot_general(
            library, other_side, (((1,), (1,)), ((), ())), preferred_element_type=jnp.float32
        )
    )
    local_best = jnp.concatenate([own_best, other_best], axis=1).T
    row = jnp.arange(local_best.shape[0], dtype=jnp.int32)
    slot = row % capacity
    source = row // capacity
    source_core = source % core_count
    source_z = source // core_count % z_count
    source_x = source // (core_count * z_count) % x_count
    source_mass = source // shard_count
    step_x = (source_x - lax.axis_index("x")) % x_count
    step_z = (source_z - lax.axis_index("z")) % z_count
    side = jnp.where(source_core == lax.axis_index("core"), 0, 1)
    in_part = source_mass * capacity + slot
    column_a = (step_z * x_count + step_x) * part + in_part
    column_b = (x_count * z_count + step_x * z_count + step_z) * part + in_part - part
    column = side * (shard_count // core_count) * 2 * part + jnp.where(in_part < part, column_a, column_b)
    outgoing = jnp.take(local_best, column, axis=0).reshape(-1, capacity, TOP_K)
    received = lax.all_to_all(
        outgoing, ("mass", "x", "z", "core"), split_axis=0, concat_axis=0, tiled=True
    )
    received = received.reshape(mass_count, shard_count, capacity, TOP_K)
    received = received.transpose(0, 2, 1, 3).reshape(mass_count * capacity, -1)
    candidates = jnp.take(received, slot_index, axis=0)
    return lax.top_k(candidates, TOP_K)[0]


def solution(mesh):
    mass_count, shard_count = mesh.devices.shape
    core_count = 2
    side = 4
    split_mesh = Mesh(
        mesh.devices.reshape(mass_count, side, shard_count // (side * core_count), core_count),
        ("mass", "x", "z", "core"),
    )
    spread = ("mass", "x", "z", "core")
    placed = (P(spread, None), P(spread, None), P(spread, None), P(spread))
    return jax.shard_map(
        per_device,
        mesh=split_mesh,
        in_specs=placed,
        out_specs=P(spread, None),
        check_vma=False,
    )
```

```python
import functools

import jax
import jax.numpy as jnp
from jax import lax
from jax.experimental import pallas as pl
from jax.experimental.pallas import tpu as pltpu
from jax.sharding import Mesh
from jax.sharding import PartitionSpec as P

MAX_SHIFT = 2048
TOP_K = 16
LANES = 128
SUBLANES = 8


def shifted_spectra(queries, offsets):
    row_count = queries.shape[0]
    bin_count = queries.shape[1]
    margin = jnp.zeros((row_count, MAX_SHIFT), queries.dtype)
    current = jnp.concatenate([margin, queries, margin], axis=1)
    window_start = MAX_SHIFT - offsets
    bit_total = (2 * MAX_SHIFT).bit_length()
    for bit_number in range(bit_total):
        step_size = 1 << bit_number
        moved = jnp.concatenate(
            [current[:, step_size:], jnp.zeros((row_count, step_size), current.dtype)], axis=1
        )
        taken = window_start >> bit_number & 1 == 1
        current = jnp.where(taken[:, None], moved, current)
    shifted = current[:, :bin_count]
    combined = queries.astype(jnp.float32) + shifted.astype(jnp.float32)
    scale_factor = lax.rsqrt(jnp.mean(combined * combined, axis=1, keepdims=True) + 1e-06)
    return (combined * scale_factor).astype(jnp.bfloat16)


def block_ranks(dest_group):
    length = dest_group.shape[0]
    position_ids = jnp.arange(length, dtype=jnp.int32)
    earlier = (dest_group[:, None] == dest_group[None, :]) & (
        position_ids[:, None] > position_ids[None, :]
    )
    return jnp.sum(earlier.astype(jnp.int32), axis=1)


def merge_sorted(first, second):
    merged = [jnp.maximum(first[k], second[TOP_K - 1 - k]) for k in range(TOP_K)]
    span = TOP_K // 2
    while span >= 1:
        for k in range(TOP_K):
            if (k // span) % 2 == 0:
                upper, lower = merged[k], merged[k + span]
                merged[k] = jnp.maximum(upper, lower)
                merged[k + span] = jnp.minimum(upper, lower)
        span //= 2
    return merged


def column_topk_kernel(scores_ref, out_ref):
    steps = scores_ref.shape[0] // SUBLANES
    lowest = jnp.full((SUBLANES, LANES), -jnp.inf, jnp.float32)

    def insert(step, kept):
        start = pl.multiple_of(step * SUBLANES, SUBLANES)
        value = scores_ref[pl.ds(start, SUBLANES), :]
        updated = []
        for k in range(TOP_K):
            updated.append(jnp.maximum(kept[k], value))
            value = jnp.minimum(kept[k], value)
        return tuple(updated)

    kept = lax.fori_loop(0, steps, insert, (lowest,) * TOP_K, unroll=8)
    kept = list(kept)
    shift = SUBLANES // 2
    while shift >= 1:
        rolled = [pltpu.roll(kept[k], shift, 0) for k in range(TOP_K)]
        kept = merge_sorted(kept, rolled)
        shift //= 2
    for k in range(TOP_K):
        out_ref[pl.ds(k, 1), :] = kept[k][0:1, :]


def column_topk(scores):
    rows, columns = scores.shape
    return pl.pallas_call(
        column_topk_kernel,
        out_shape=jax.ShapeDtypeStruct((TOP_K, columns), jnp.float32),
        grid=(columns // LANES,),
        in_specs=[pl.BlockSpec((rows, LANES), lambda j: (0, j))],
        out_specs=pl.BlockSpec((TOP_K, LANES), lambda j: (0, j)),
        cost_estimate=pl.CostEstimate(
            flops=2 * TOP_K * rows * columns, transcendentals=0, bytes_accessed=4 * rows * columns
        ),
    )(scores)


LIB_BLOCK = 256
BIN_BLOCK = 1024


def score_topk_kernel(library_ref, first_ref, second_ref, out_ref, scores_ref, kept_ref):
    block = pl.program_id(0)
    slots = first_ref.shape[0]
    bins = first_ref.shape[1]

    @pl.when(block == 0)
    def _():
        kept_ref[...] = jnp.full(kept_ref.shape, -jnp.inf, jnp.float32)

    for piece, query_ref in enumerate((first_ref, second_ref)):
        scores_ref[...] = jnp.zeros(scores_ref.shape, jnp.float32)

        def accumulate(chunk, carry):
            lo = pl.multiple_of(chunk * BIN_BLOCK, BIN_BLOCK)
            scores_ref[...] += lax.dot_general(
                library_ref[:, pl.ds(lo, BIN_BLOCK)],
                query_ref[:, pl.ds(lo, BIN_BLOCK)],
                (((1,), (1,)), ((), ())),
                preferred_element_type=jnp.float32,
            )
            return carry

        lax.fori_loop(0, bins // BIN_BLOCK, accumulate, 0)
        for lane_block in range(slots // LANES):
            insert_rows_at(scores_ref, kept_ref, lane_block * LANES, piece * slots + lane_block * LANES)

    @pl.when(block == pl.num_programs(0) - 1)
    def _():
        for column in range(0, 2 * slots, LANES):
            lanes = pl.ds(column, LANES)
            kept = [kept_ref[k, :, lanes] for k in range(TOP_K)]
            shift = SUBLANES // 2
            while shift >= 1:
                rolled = [pltpu.roll(kept[k], shift, 0) for k in range(TOP_K)]
                kept = merge_sorted(kept, rolled)
                shift //= 2
            for k in range(TOP_K):
                out_ref[pl.ds(k, 1), lanes] = kept[k][0:1, :]


def insert_rows_at(scores_ref, kept_ref, score_column, kept_column):
    score_lanes = pl.ds(score_column, LANES)
    kept_lanes = pl.ds(kept_column, LANES)
    kept = tuple(kept_ref[k, :, kept_lanes] for k in range(TOP_K))

    def insert(step, kept):
        start = pl.multiple_of(step * SUBLANES, SUBLANES)
        value = scores_ref[pl.ds(start, SUBLANES), score_lanes]
        updated = []
        for k in range(TOP_K):
            updated.append(jnp.maximum(kept[k], value))
            value = jnp.minimum(kept[k], value)
        return tuple(updated)

    kept = lax.fori_loop(0, scores_ref.shape[0] // SUBLANES, insert, kept, unroll=8)
    for k in range(TOP_K):
        kept_ref[k, :, kept_lanes] = kept[k]


def score_topk(library, first, second):
    rows, bins = library.shape
    slots = first.shape[0]
    resident = lambda block: (0, 0)
    return pl.pallas_call(
        score_topk_kernel,
        out_shape=jax.ShapeDtypeStruct((TOP_K, 2 * slots), jnp.float32),
        grid=(rows // LIB_BLOCK,),
        in_specs=[
            pl.BlockSpec((LIB_BLOCK, bins), lambda block: (block, 0)),
            pl.BlockSpec((slots, bins), resident, pipeline_mode=pl.Buffered(1)),
            pl.BlockSpec((slots, bins), resident, pipeline_mode=pl.Buffered(1)),
        ],
        out_specs=pl.BlockSpec((TOP_K, 2 * slots), resident),
        scratch_shapes=[
            pltpu.VMEM((LIB_BLOCK, slots), jnp.float32),
            pltpu.VMEM((TOP_K, SUBLANES, 2 * slots), jnp.float32),
        ],
        compiler_params=pltpu.CompilerParams(
            dimension_semantics=("arbitrary",), vmem_limit_bytes=48 * 1024 * 1024
        ),
        cost_estimate=pl.CostEstimate(
            flops=2 * rows * 2 * slots * bins,
            transcendentals=0,
            bytes_accessed=2 * rows * bins + 2 * 2 * slots * bins,
        ),
    )(library, first, second)


def ring_gather(block, axis):
    size = 4
    flat = block.reshape(-1, block.shape[-1])
    half = flat.shape[0] // 2
    forward = [(i, (i + 1) % size) for i in range(size)]
    backward = [(i, (i - 1) % size) for i in range(size)]
    from_minus = lax.ppermute(flat, axis, forward)
    from_plus = lax.ppermute(flat, axis, backward)
    far_first = lax.ppermute(from_minus[:half], axis, forward)
    far_second = lax.ppermute(from_plus[half:], axis, backward)
    far = jnp.concatenate([far_first, far_second], axis=0)
    stacked = jnp.stack([flat, from_plus, far, from_minus])
    return stacked.reshape((size,) + block.shape)


def per_device(queries, library, routes, offsets):
    mass_count = lax.axis_size("mass")
    x_count = lax.axis_size("x")
    z_count = lax.axis_size("z")
    core_count = lax.axis_size("core")
    shard_count = x_count * z_count * core_count
    query_count = queries.shape[0]
    capacity = query_count // 2
    spectra = shifted_spectra(queries, offsets)
    dest_group = routes[:, 0]
    slot_index = dest_group * capacity + block_ranks(dest_group)
    selector = (
        jnp.arange(mass_count * capacity, dtype=jnp.int32)[:, None] == slot_index[None, :]
    ).astype(jnp.bfloat16)
    packed = jnp.dot(selector, spectra, preferred_element_type=jnp.float32).astype(jnp.bfloat16)
    arrived = lax.all_to_all(packed, "mass", split_axis=0, concat_axis=0, tiled=True)
    part = arrived.shape[0] // 2
    part_a = ring_gather(ring_gather(arrived[:part], "x"), "z")
    part_b = ring_gather(ring_gather(arrived[part:], "z"), "x")
    bins = arrived.shape[1]
    own_a = part_a.reshape(-1, bins)
    own_b = part_b.reshape(-1, bins)
    partner = [(core, core_count - 1 - core) for core in range(core_count)]
    other_a = lax.ppermute(own_a, "core", partner)
    other_b = lax.ppermute(own_b, "core", partner)
    own_best = score_topk(library, own_a, own_b)
    other_best = score_topk(library, other_a, other_b)
    local_best = jnp.concatenate([own_best, other_best], axis=1).T
    row = jnp.arange(local_best.shape[0], dtype=jnp.int32)
    slot = row % capacity
    source = row // capacity
    source_core = source % core_count
    source_z = source // core_count % z_count
    source_x = source // (core_count * z_count) % x_count
    source_mass = source // shard_count
    step_x = (source_x - lax.axis_index("x")) % x_count
    step_z = (source_z - lax.axis_index("z")) % z_count
    side = jnp.where(source_core == lax.axis_index("core"), 0, 1)
    in_part = source_mass * capacity + slot
    column_a = (step_z * x_count + step_x) * part + in_part
    column_b = (x_count * z_count + step_x * z_count + step_z) * part + in_part - part
    column = side * (shard_count // core_count) * 2 * part + jnp.where(in_part < part, column_a, column_b)
    outgoing = jnp.take(local_best, column, axis=0).reshape(-1, capacity, TOP_K)
    received = lax.all_to_all(
        outgoing, ("mass", "x", "z", "core"), split_axis=0, concat_axis=0, tiled=True
    )
    received = received.reshape(mass_count, shard_count, capacity, TOP_K)
    received = received.transpose(0, 2, 1, 3).reshape(mass_count * capacity, -1)
    candidates = jnp.take(received, slot_index, axis=0)
    return lax.top_k(candidates, TOP_K)[0]


def solution(mesh):
    mass_count, shard_count = mesh.devices.shape
    core_count = 2
    side = 4
    split_mesh = Mesh(
        mesh.devices.reshape(mass_count, side, shard_count // (side * core_count), core_count),
        ("mass", "x", "z", "core"),
    )
    spread = ("mass", "x", "z", "core")
    placed = (P(spread, None), P(spread, None), P(spread, None), P(spread))
    return jax.shard_map(
        per_device,
        mesh=split_mesh,
        in_specs=placed,
        out_specs=P(spread, None),
        check_vma=False,
    )
```

```python
import functools

import jax
import jax.numpy as jnp
from jax import lax
from jax.experimental import pallas as pl
from jax.experimental.pallas import tpu as pltpu
from jax.sharding import Mesh
from jax.sharding import PartitionSpec as P

MAX_SHIFT = 2048
TOP_K = 16
LANES = 128
SUBLANES = 8


def shifted_spectra(queries, offsets):
    row_count = queries.shape[0]
    bin_count = queries.shape[1]
    margin = jnp.zeros((row_count, MAX_SHIFT), queries.dtype)
    current = jnp.concatenate([margin, queries, margin], axis=1)
    window_start = MAX_SHIFT - offsets
    bit_total = (2 * MAX_SHIFT).bit_length()
    for bit_number in range(bit_total):
        step_size = 1 << bit_number
        moved = jnp.concatenate(
            [current[:, step_size:], jnp.zeros((row_count, step_size), current.dtype)], axis=1
        )
        taken = window_start >> bit_number & 1 == 1
        current = jnp.where(taken[:, None], moved, current)
    shifted = current[:, :bin_count]
    combined = queries.astype(jnp.float32) + shifted.astype(jnp.float32)
    scale_factor = lax.rsqrt(jnp.mean(combined * combined, axis=1, keepdims=True) + 1e-06)
    return (combined * scale_factor).astype(jnp.bfloat16)


def block_ranks(dest_group):
    length = dest_group.shape[0]
    position_ids = jnp.arange(length, dtype=jnp.int32)
    earlier = (dest_group[:, None] == dest_group[None, :]) & (
        position_ids[:, None] > position_ids[None, :]
    )
    return jnp.sum(earlier.astype(jnp.int32), axis=1)


def merge_sorted(first, second):
    merged = [jnp.maximum(first[k], second[TOP_K - 1 - k]) for k in range(TOP_K)]
    span = TOP_K // 2
    while span >= 1:
        for k in range(TOP_K):
            if (k // span) % 2 == 0:
                upper, lower = merged[k], merged[k + span]
                merged[k] = jnp.maximum(upper, lower)
                merged[k + span] = jnp.minimum(upper, lower)
        span //= 2
    return merged


def column_topk_kernel(scores_ref, out_ref):
    steps = scores_ref.shape[0] // SUBLANES
    lowest = jnp.full((SUBLANES, LANES), -jnp.inf, jnp.float32)

    def insert(step, kept):
        start = pl.multiple_of(step * SUBLANES, SUBLANES)
        value = scores_ref[pl.ds(start, SUBLANES), :]
        updated = []
        for k in range(TOP_K):
            updated.append(jnp.maximum(kept[k], value))
            value = jnp.minimum(kept[k], value)
        return tuple(updated)

    kept = lax.fori_loop(0, steps, insert, (lowest,) * TOP_K, unroll=8)
    kept = list(kept)
    shift = SUBLANES // 2
    while shift >= 1:
        rolled = [pltpu.roll(kept[k], shift, 0) for k in range(TOP_K)]
        kept = merge_sorted(kept, rolled)
        shift //= 2
    for k in range(TOP_K):
        out_ref[pl.ds(k, 1), :] = kept[k][0:1, :]


def column_topk(scores):
    rows, columns = scores.shape
    return pl.pallas_call(
        column_topk_kernel,
        out_shape=jax.ShapeDtypeStruct((TOP_K, columns), jnp.float32),
        grid=(columns // LANES,),
        in_specs=[pl.BlockSpec((rows, LANES), lambda j: (0, j))],
        out_specs=pl.BlockSpec((TOP_K, LANES), lambda j: (0, j)),
        cost_estimate=pl.CostEstimate(
            flops=2 * TOP_K * rows * columns, transcendentals=0, bytes_accessed=4 * rows * columns
        ),
    )(scores)


def ring_gather(block, axis):
    size = 4
    flat = block.reshape(-1, block.shape[-1])
    half = flat.shape[0] // 2
    forward = [(i, (i + 1) % size) for i in range(size)]
    backward = [(i, (i - 1) % size) for i in range(size)]
    from_minus = lax.ppermute(flat, axis, forward)
    from_plus = lax.ppermute(flat, axis, backward)
    far_first = lax.ppermute(from_minus[:half], axis, forward)
    far_second = lax.ppermute(from_plus[half:], axis, backward)
    far = jnp.concatenate([far_first, far_second], axis=0)
    stacked = jnp.stack([flat, from_plus, far, from_minus])
    return stacked.reshape((size,) + block.shape)


def per_device(queries, library, routes, offsets):
    mass_count = lax.axis_size("mass")
    x_count = lax.axis_size("x")
    z_count = lax.axis_size("z")
    core_count = lax.axis_size("core")
    shard_count = x_count * z_count * core_count
    query_count = queries.shape[0]
    capacity = query_count // 2
    spectra = shifted_spectra(queries, offsets)
    dest_group = routes[:, 0]
    slot_index = dest_group * capacity + block_ranks(dest_group)
    selector = (
        jnp.arange(mass_count * capacity, dtype=jnp.int32)[:, None] == slot_index[None, :]
    ).astype(jnp.bfloat16)
    packed = jnp.dot(selector, spectra, preferred_element_type=jnp.float32).astype(jnp.bfloat16)
    packed = packed.reshape(mass_count, capacity, packed.shape[-1])
    own_mass = lax.axis_index("mass")
    chunks = []
    for distance in range(mass_count):
        outgoing = jnp.take(packed, (own_mass + distance) % mass_count, axis=0)
        if distance:
            outgoing = lax.ppermute(
                outgoing,
                "mass",
                [(source, (source + distance) % mass_count) for source in range(mass_count)],
            )
        chunks.append(outgoing)
    arrived = jnp.concatenate(chunks, axis=0)
    part = arrived.shape[0] // 2
    part_a = ring_gather(ring_gather(arrived[:part], "x"), "z")
    part_b = ring_gather(ring_gather(arrived[part:], "z"), "x")
    own_side = jnp.concatenate(
        [part_a.reshape(-1, arrived.shape[1]), part_b.reshape(-1, arrived.shape[1])], axis=0
    )
    partner = [(core, core_count - 1 - core) for core in range(core_count)]
    other_side = lax.ppermute(own_side, "core", partner)
    own_best = column_topk(
        lax.dot_general(
            library, own_side, (((1,), (1,)), ((), ())), preferred_element_type=jnp.float32
        )
    )
    other_best = column_topk(
        lax.dot_general(
            library, other_side, (((1,), (1,)), ((), ())), preferred_element_type=jnp.float32
        )
    )
    local_best = jnp.concatenate([own_best, other_best], axis=1).T
    row = jnp.arange(local_best.shape[0], dtype=jnp.int32)
    slot = row % capacity
    source = row // capacity
    source_core = source % core_count
    source_z = source // core_count % z_count
    source_x = source // (core_count * z_count) % x_count
    source_mass = source // shard_count
    step_x = (source_x - lax.axis_index("x")) % x_count
    step_z = (source_z - lax.axis_index("z")) % z_count
    side = jnp.where(source_core == lax.axis_index("core"), 0, 1)
    in_part = (own_mass - source_mass) % mass_count * capacity + slot
    column_a = (step_z * x_count + step_x) * part + in_part
    column_b = (x_count * z_count + step_x * z_count + step_z) * part + in_part - part
    column = side * (shard_count // core_count) * 2 * part + jnp.where(in_part < part, column_a, column_b)
    outgoing = jnp.take(local_best, column, axis=0).reshape(-1, capacity, TOP_K)
    received = lax.all_to_all(
        outgoing, ("mass", "x", "z", "core"), split_axis=0, concat_axis=0, tiled=True
    )
    received = received.reshape(mass_count, shard_count, capacity, TOP_K)
    received = received.transpose(0, 2, 1, 3).reshape(mass_count * capacity, -1)
    candidates = jnp.take(received, slot_index, axis=0)
    return lax.top_k(candidates, TOP_K)[0]


def solution(mesh):
    mass_count, shard_count = mesh.devices.shape
    core_count = 2
    side = 4
    split_mesh = Mesh(
        mesh.devices.reshape(mass_count, side, shard_count // (side * core_count), core_count),
        ("mass", "x", "z", "core"),
    )
    spread = ("mass", "x", "z", "core")
    placed = (P(spread, None), P(spread, None), P(spread, None), P(spread))
    return jax.shard_map(
        per_device,
        mesh=split_mesh,
        in_specs=placed,
        out_specs=P(spread, None),
        check_vma=False,
    )
```

```python
import functools

import jax
import jax.numpy as jnp
from jax import lax
from jax.experimental import pallas as pl
from jax.experimental.pallas import tpu as pltpu
from jax.sharding import Mesh
from jax.sharding import PartitionSpec as P

MAX_SHIFT = 2048
TOP_K = 16
LANES = 128
SUBLANES = 8


def shifted_spectra(queries, offsets):
    row_count = queries.shape[0]
    bin_count = queries.shape[1]
    margin = jnp.zeros((row_count, MAX_SHIFT), queries.dtype)
    current = jnp.concatenate([margin, queries, margin], axis=1)
    window_start = MAX_SHIFT - offsets
    bit_total = (2 * MAX_SHIFT).bit_length()
    for bit_number in range(bit_total):
        step_size = 1 << bit_number
        moved = jnp.concatenate(
            [current[:, step_size:], jnp.zeros((row_count, step_size), current.dtype)], axis=1
        )
        taken = window_start >> bit_number & 1 == 1
        current = jnp.where(taken[:, None], moved, current)
    shifted = current[:, :bin_count]
    combined = queries.astype(jnp.float32) + shifted.astype(jnp.float32)
    scale_factor = lax.rsqrt(jnp.mean(combined * combined, axis=1, keepdims=True) + 1e-06)
    return (combined * scale_factor).astype(jnp.bfloat16)


def block_ranks(dest_group):
    length = dest_group.shape[0]
    position_ids = jnp.arange(length, dtype=jnp.int32)
    earlier = (dest_group[:, None] == dest_group[None, :]) & (
        position_ids[:, None] > position_ids[None, :]
    )
    return jnp.sum(earlier.astype(jnp.int32), axis=1)


def merge_sorted(first, second):
    merged = [jnp.maximum(first[k], second[TOP_K - 1 - k]) for k in range(TOP_K)]
    span = TOP_K // 2
    while span >= 1:
        for k in range(TOP_K):
            if (k // span) % 2 == 0:
                upper, lower = merged[k], merged[k + span]
                merged[k] = jnp.maximum(upper, lower)
                merged[k + span] = jnp.minimum(upper, lower)
        span //= 2
    return merged


def column_topk_kernel(scores_ref, out_ref):
    steps = scores_ref.shape[0] // SUBLANES
    lowest = jnp.full((SUBLANES, LANES), -jnp.inf, jnp.float32)

    def insert(step, kept):
        start = pl.multiple_of(step * SUBLANES, SUBLANES)
        value = scores_ref[pl.ds(start, SUBLANES), :]
        updated = []
        for k in range(TOP_K):
            updated.append(jnp.maximum(kept[k], value))
            value = jnp.minimum(kept[k], value)
        return tuple(updated)

    kept = lax.fori_loop(0, steps, insert, (lowest,) * TOP_K, unroll=8)
    kept = list(kept)
    shift = SUBLANES // 2
    while shift >= 1:
        rolled = [pltpu.roll(kept[k], shift, 0) for k in range(TOP_K)]
        kept = merge_sorted(kept, rolled)
        shift //= 2
    for k in range(TOP_K):
        out_ref[pl.ds(k, 1), :] = kept[k][0:1, :]


def column_topk(scores):
    rows, columns = scores.shape
    return pl.pallas_call(
        column_topk_kernel,
        out_shape=jax.ShapeDtypeStruct((TOP_K, columns), jnp.float32),
        grid=(columns // LANES,),
        in_specs=[pl.BlockSpec((rows, LANES), lambda j: (0, j))],
        out_specs=pl.BlockSpec((TOP_K, LANES), lambda j: (0, j)),
        cost_estimate=pl.CostEstimate(
            flops=2 * TOP_K * rows * columns, transcendentals=0, bytes_accessed=4 * rows * columns
        ),
    )(scores)


def ring_gather(block, axis):
    size = 4
    flat = block.reshape(-1, block.shape[-1])
    half = flat.shape[0] // 2
    forward = [(i, (i + 1) % size) for i in range(size)]
    backward = [(i, (i - 1) % size) for i in range(size)]
    from_minus = lax.ppermute(flat, axis, forward)
    from_plus = lax.ppermute(flat, axis, backward)
    far_first = lax.ppermute(from_minus[:half], axis, forward)
    far_second = lax.ppermute(from_plus[half:], axis, backward)
    return [flat, from_plus, far_first, far_second, from_minus]


def stacked_ring(block, axis):
    return jnp.concatenate(ring_gather(block, axis), axis=0).reshape((4,) + block.shape)


def per_device(queries, library, routes, offsets):
    mass_count = lax.axis_size("mass")
    x_count = lax.axis_size("x")
    z_count = lax.axis_size("z")
    core_count = lax.axis_size("core")
    shard_count = x_count * z_count * core_count
    query_count = queries.shape[0]
    capacity = query_count // 2
    spectra = shifted_spectra(queries, offsets)
    dest_group = routes[:, 0]
    slot_index = dest_group * capacity + block_ranks(dest_group)
    selector = (
        jnp.arange(mass_count * capacity, dtype=jnp.int32)[:, None] == slot_index[None, :]
    ).astype(jnp.bfloat16)
    packed = jnp.dot(selector, spectra, preferred_element_type=jnp.float32).astype(jnp.bfloat16)
    packed = packed.reshape(mass_count, capacity, packed.shape[-1])
    own_mass = lax.axis_index("mass")
    chunks = []
    for distance in range(mass_count):
        outgoing = jnp.take(packed, (own_mass + distance) % mass_count, axis=0)
        if distance:
            outgoing = lax.ppermute(
                outgoing,
                "mass",
                [(source, (source + distance) % mass_count) for source in range(mass_count)],
            )
        chunks.append(outgoing)
    arrived = jnp.concatenate(chunks, axis=0)
    part = arrived.shape[0] // 2
    pieces_a = ring_gather(stacked_ring(arrived[:part], "x"), "z")
    pieces_b = ring_gather(stacked_ring(arrived[part:], "z"), "x")
    own_side = jnp.concatenate(pieces_a + pieces_b, axis=0)
    partner = [(core, core_count - 1 - core) for core in range(core_count)]
    other_side = lax.ppermute(own_side, "core", partner)
    own_best = column_topk(
        lax.dot_general(
            library, own_side, (((1,), (1,)), ((), ())), preferred_element_type=jnp.float32
        )
    )
    other_best = column_topk(
        lax.dot_general(
            library, other_side, (((1,), (1,)), ((), ())), preferred_element_type=jnp.float32
        )
    )
    local_best = jnp.concatenate([own_best, other_best], axis=1).T
    row = jnp.arange(local_best.shape[0], dtype=jnp.int32)
    slot = row % capacity
    source = row // capacity
    source_core = source % core_count
    source_z = source // core_count % z_count
    source_x = source // (core_count * z_count) % x_count
    source_mass = source // shard_count
    step_x = (source_x - lax.axis_index("x")) % x_count
    step_z = (source_z - lax.axis_index("z")) % z_count
    side = jnp.where(source_core == lax.axis_index("core"), 0, 1)
    in_part = (own_mass - source_mass) % mass_count * capacity + slot
    column_a = (step_z * x_count + step_x) * part + in_part
    column_b = (x_count * z_count + step_x * z_count + step_z) * part + in_part - part
    column = side * (shard_count // core_count) * 2 * part + jnp.where(in_part < part, column_a, column_b)
    outgoing = jnp.take(local_best, column, axis=0).reshape(-1, capacity, TOP_K)
    received = lax.all_to_all(
        outgoing, ("mass", "x", "z", "core"), split_axis=0, concat_axis=0, tiled=True
    )
    received = received.reshape(mass_count, shard_count, capacity, TOP_K)
    received = received.transpose(0, 2, 1, 3).reshape(mass_count * capacity, -1)
    candidates = jnp.take(received, slot_index, axis=0)
    return lax.top_k(candidates, TOP_K)[0]


def solution(mesh):
    mass_count, shard_count = mesh.devices.shape
    core_count = 2
    side = 4
    split_mesh = Mesh(
        mesh.devices.reshape(mass_count, side, shard_count // (side * core_count), core_count),
        ("mass", "x", "z", "core"),
    )
    spread = ("mass", "x", "z", "core")
    placed = (P(spread, None), P(spread, None), P(spread, None), P(spread))
    return jax.shard_map(
        per_device,
        mesh=split_mesh,
        in_specs=placed,
        out_specs=P(spread, None),
        check_vma=False,
    )
```

```python
import functools

import jax
import jax.numpy as jnp
from jax import lax
from jax.experimental import pallas as pl
from jax.experimental.pallas import tpu as pltpu
from jax.sharding import Mesh
from jax.sharding import PartitionSpec as P

MAX_SHIFT = 2048
TOP_K = 16
LANES = 128
SUBLANES = 8


def shifted_spectra(queries, offsets):
    row_count = queries.shape[0]
    bin_count = queries.shape[1]
    margin = jnp.zeros((row_count, MAX_SHIFT), queries.dtype)
    current = jnp.concatenate([margin, queries, margin], axis=1)
    window_start = MAX_SHIFT - offsets
    bit_total = (2 * MAX_SHIFT).bit_length()
    for bit_number in range(bit_total):
        step_size = 1 << bit_number
        moved = jnp.concatenate(
            [current[:, step_size:], jnp.zeros((row_count, step_size), current.dtype)], axis=1
        )
        taken = window_start >> bit_number & 1 == 1
        current = jnp.where(taken[:, None], moved, current)
    shifted = current[:, :bin_count]
    combined = queries.astype(jnp.float32) + shifted.astype(jnp.float32)
    scale_factor = lax.rsqrt(jnp.mean(combined * combined, axis=1, keepdims=True) + 1e-06)
    return (combined * scale_factor).astype(jnp.bfloat16)


def block_ranks(dest_group):
    length = dest_group.shape[0]
    position_ids = jnp.arange(length, dtype=jnp.int32)
    earlier = (dest_group[:, None] == dest_group[None, :]) & (
        position_ids[:, None] > position_ids[None, :]
    )
    return jnp.sum(earlier.astype(jnp.int32), axis=1)


def merge_sorted(first, second):
    merged = [jnp.maximum(first[k], second[TOP_K - 1 - k]) for k in range(TOP_K)]
    span = TOP_K // 2
    while span >= 1:
        for k in range(TOP_K):
            if (k // span) % 2 == 0:
                upper, lower = merged[k], merged[k + span]
                merged[k] = jnp.maximum(upper, lower)
                merged[k + span] = jnp.minimum(upper, lower)
        span //= 2
    return merged


def bitonic_sort(values):
    values = list(values)
    width = 2
    while width <= TOP_K:
        span = width // 2
        while span >= 1:
            for i in range(TOP_K):
                j = i ^ span
                if j > i:
                    high = jnp.maximum(values[i], values[j])
                    low = jnp.minimum(values[i], values[j])
                    if i & width == 0:
                        values[i], values[j] = high, low
                    else:
                        values[i], values[j] = low, high
            span //= 2
        width *= 2
    return values


def column_topk_kernel(scores_ref, out_ref):
    group = SUBLANES * TOP_K
    steps = scores_ref.shape[0] // group
    lowest = jnp.full((SUBLANES, LANES), -jnp.inf, jnp.float32)

    def insert(step, kept):
        start = pl.multiple_of(step * group, group)
        values = [scores_ref[pl.ds(start + SUBLANES * k, SUBLANES), :] for k in range(TOP_K)]
        return tuple(merge_sorted(list(kept), bitonic_sort(values)))

    kept = lax.fori_loop(0, steps, insert, (lowest,) * TOP_K, unroll=2)
    kept = list(kept)
    shift = SUBLANES // 2
    while shift >= 1:
        rolled = [pltpu.roll(kept[k], shift, 0) for k in range(TOP_K)]
        kept = merge_sorted(kept, rolled)
        shift //= 2
    for k in range(TOP_K):
        out_ref[pl.ds(k, 1), :] = kept[k][0:1, :]


def column_topk(scores):
    rows, columns = scores.shape
    return pl.pallas_call(
        column_topk_kernel,
        out_shape=jax.ShapeDtypeStruct((TOP_K, columns), jnp.float32),
        grid=(columns // LANES,),
        in_specs=[pl.BlockSpec((rows, LANES), lambda j: (0, j))],
        out_specs=pl.BlockSpec((TOP_K, LANES), lambda j: (0, j)),
        cost_estimate=pl.CostEstimate(
            flops=2 * TOP_K * rows * columns, transcendentals=0, bytes_accessed=4 * rows * columns
        ),
    )(scores)


def ring_gather(block, axis):
    size = 4
    flat = block.reshape(-1, block.shape[-1])
    half = flat.shape[0] // 2
    forward = [(i, (i + 1) % size) for i in range(size)]
    backward = [(i, (i - 1) % size) for i in range(size)]
    from_minus = lax.ppermute(flat, axis, forward)
    from_plus = lax.ppermute(flat, axis, backward)
    far_first = lax.ppermute(from_minus[:half], axis, forward)
    far_second = lax.ppermute(from_plus[half:], axis, backward)
    far = jnp.concatenate([far_first, far_second], axis=0)
    stacked = jnp.stack([flat, from_plus, far, from_minus])
    return stacked.reshape((size,) + block.shape)


def per_device(queries, library, routes, offsets):
    mass_count = lax.axis_size("mass")
    x_count = lax.axis_size("x")
    z_count = lax.axis_size("z")
    core_count = lax.axis_size("core")
    shard_count = x_count * z_count * core_count
    query_count = queries.shape[0]
    capacity = query_count // 2
    spectra = shifted_spectra(queries, offsets)
    dest_group = routes[:, 0]
    slot_index = dest_group * capacity + block_ranks(dest_group)
    selector = (
        jnp.arange(mass_count * capacity, dtype=jnp.int32)[:, None] == slot_index[None, :]
    ).astype(jnp.bfloat16)
    packed = jnp.dot(selector, spectra, preferred_element_type=jnp.float32).astype(jnp.bfloat16)
    packed = packed.reshape(mass_count, capacity, packed.shape[-1])
    own_mass = lax.axis_index("mass")
    chunks = []
    for distance in range(mass_count):
        outgoing = jnp.take(packed, (own_mass + distance) % mass_count, axis=0)
        if distance:
            outgoing = lax.ppermute(
                outgoing,
                "mass",
                [(source, (source + distance) % mass_count) for source in range(mass_count)],
            )
        chunks.append(outgoing)
    arrived = jnp.concatenate(chunks, axis=0)
    part = arrived.shape[0] // 2
    part_a = ring_gather(ring_gather(arrived[:part], "x"), "z")
    part_b = ring_gather(ring_gather(arrived[part:], "z"), "x")
    own_side = jnp.concatenate(
        [part_a.reshape(-1, arrived.shape[1]), part_b.reshape(-1, arrived.shape[1])], axis=0
    )
    partner = [(core, core_count - 1 - core) for core in range(core_count)]
    other_side = lax.ppermute(own_side, "core", partner)
    own_best = column_topk(
        lax.dot_general(
            library, own_side, (((1,), (1,)), ((), ())), preferred_element_type=jnp.float32
        )
    )
    other_best = column_topk(
        lax.dot_general(
            library, other_side, (((1,), (1,)), ((), ())), preferred_element_type=jnp.float32
        )
    )
    local_best = jnp.concatenate([own_best, other_best], axis=1).T
    row = jnp.arange(local_best.shape[0], dtype=jnp.int32)
    slot = row % capacity
    source = row // capacity
    source_core = source % core_count
    source_z = source // core_count % z_count
    source_x = source // (core_count * z_count) % x_count
    source_mass = source // shard_count
    step_x = (source_x - lax.axis_index("x")) % x_count
    step_z = (source_z - lax.axis_index("z")) % z_count
    side = jnp.where(source_core == lax.axis_index("core"), 0, 1)
    in_part = (own_mass - source_mass) % mass_count * capacity + slot
    column_a = (step_z * x_count + step_x) * part + in_part
    column_b = (x_count * z_count + step_x * z_count + step_z) * part + in_part - part
    column = side * (shard_count // core_count) * 2 * part + jnp.where(in_part < part, column_a, column_b)
    outgoing = jnp.take(local_best, column, axis=0).reshape(-1, capacity, TOP_K)
    received = lax.all_to_all(
        outgoing, ("mass", "x", "z", "core"), split_axis=0, concat_axis=0, tiled=True
    )
    received = received.reshape(mass_count, shard_count, capacity, TOP_K)
    received = received.transpose(0, 2, 1, 3).reshape(mass_count * capacity, -1)
    candidates = jnp.take(received, slot_index, axis=0)
    return lax.top_k(candidates, TOP_K)[0]


def solution(mesh):
    mass_count, shard_count = mesh.devices.shape
    core_count = 2
    side = 4
    split_mesh = Mesh(
        mesh.devices.reshape(mass_count, side, shard_count // (side * core_count), core_count),
        ("mass", "x", "z", "core"),
    )
    spread = ("mass", "x", "z", "core")
    placed = (P(spread, None), P(spread, None), P(spread, None), P(spread))
    return jax.shard_map(
        per_device,
        mesh=split_mesh,
        in_specs=placed,
        out_specs=P(spread, None),
        check_vma=False,
    )
```

```python
import functools

import jax
import jax.numpy as jnp
from jax import lax
from jax.experimental import pallas as pl
from jax.experimental.pallas import tpu as pltpu
from jax.sharding import Mesh
from jax.sharding import PartitionSpec as P

MAX_SHIFT = 2048
TOP_K = 16
LANES = 128
SUBLANES = 8


def shifted_spectra(queries, offsets):
    row_count = queries.shape[0]
    bin_count = queries.shape[1]
    margin = jnp.zeros((row_count, MAX_SHIFT), queries.dtype)
    current = jnp.concatenate([margin, queries, margin], axis=1)
    window_start = MAX_SHIFT - offsets
    position = 0
    while (1 << position) <= 2 * MAX_SHIFT:
        step_size = 1 << position
        digit = window_start >> position & 3
        result = current
        for multiple in (1, 2, 3):
            amount = multiple * step_size
            if amount > 2 * MAX_SHIFT:
                break
            moved = jnp.concatenate(
                [current[:, amount:], jnp.zeros((row_count, amount), current.dtype)], axis=1
            )
            result = jnp.where((digit == multiple)[:, None], moved, result)
        current = result
        position += 2
    shifted = current[:, :bin_count]
    combined = queries.astype(jnp.float32) + shifted.astype(jnp.float32)
    scale_factor = lax.rsqrt(jnp.mean(combined * combined, axis=1, keepdims=True) + 1e-06)
    return (combined * scale_factor).astype(jnp.bfloat16)


def block_ranks(dest_group):
    length = dest_group.shape[0]
    position_ids = jnp.arange(length, dtype=jnp.int32)
    earlier = (dest_group[:, None] == dest_group[None, :]) & (
        position_ids[:, None] > position_ids[None, :]
    )
    return jnp.sum(earlier.astype(jnp.int32), axis=1)


def merge_sorted(first, second):
    merged = [jnp.maximum(first[k], second[TOP_K - 1 - k]) for k in range(TOP_K)]
    span = TOP_K // 2
    while span >= 1:
        for k in range(TOP_K):
            if (k // span) % 2 == 0:
                upper, lower = merged[k], merged[k + span]
                merged[k] = jnp.maximum(upper, lower)
                merged[k + span] = jnp.minimum(upper, lower)
        span //= 2
    return merged


def bitonic_sort(values):
    values = list(values)
    width = 2
    while width <= TOP_K:
        span = width // 2
        while span >= 1:
            for i in range(TOP_K):
                j = i ^ span
                if j > i:
                    high = jnp.maximum(values[i], values[j])
                    low = jnp.minimum(values[i], values[j])
                    if i & width == 0:
                        values[i], values[j] = high, low
                    else:
                        values[i], values[j] = low, high
            span //= 2
        width *= 2
    return values


def column_topk_kernel(scores_ref, out_ref):
    group = SUBLANES * TOP_K
    steps = scores_ref.shape[0] // group
    lowest = jnp.full((SUBLANES, LANES), -jnp.inf, jnp.float32)

    def insert(step, kept):
        start = pl.multiple_of(step * group, group)
        values = [scores_ref[pl.ds(start + SUBLANES * k, SUBLANES), :] for k in range(TOP_K)]
        return tuple(merge_sorted(list(kept), bitonic_sort(values)))

    kept = lax.fori_loop(0, steps, insert, (lowest,) * TOP_K, unroll=2)
    kept = list(kept)
    shift = SUBLANES // 2
    while shift >= 1:
        rolled = [pltpu.roll(kept[k], shift, 0) for k in range(TOP_K)]
        kept = merge_sorted(kept, rolled)
        shift //= 2
    for k in range(TOP_K):
        out_ref[pl.ds(k, 1), :] = kept[k][0:1, :]


def column_topk(scores):
    rows, columns = scores.shape
    return pl.pallas_call(
        column_topk_kernel,
        out_shape=jax.ShapeDtypeStruct((TOP_K, columns), jnp.float32),
        grid=(columns // LANES,),
        in_specs=[pl.BlockSpec((rows, LANES), lambda j: (0, j))],
        out_specs=pl.BlockSpec((TOP_K, LANES), lambda j: (0, j)),
        cost_estimate=pl.CostEstimate(
            flops=2 * TOP_K * rows * columns, transcendentals=0, bytes_accessed=4 * rows * columns
        ),
    )(scores)


def ring_gather(block, axis):
    size = 4
    flat = block.reshape(-1, block.shape[-1])
    half = flat.shape[0] // 2
    forward = [(i, (i + 1) % size) for i in range(size)]
    backward = [(i, (i - 1) % size) for i in range(size)]
    from_minus = lax.ppermute(flat, axis, forward)
    from_plus = lax.ppermute(flat, axis, backward)
    far_first = lax.ppermute(from_minus[:half], axis, forward)
    far_second = lax.ppermute(from_plus[half:], axis, backward)
    far = jnp.concatenate([far_first, far_second], axis=0)
    stacked = jnp.stack([flat, from_plus, far, from_minus])
    return stacked.reshape((size,) + block.shape)


def per_device(queries, library, routes, offsets):
    mass_count = lax.axis_size("mass")
    x_count = lax.axis_size("x")
    z_count = lax.axis_size("z")
    core_count = lax.axis_size("core")
    shard_count = x_count * z_count * core_count
    query_count = queries.shape[0]
    capacity = query_count // 2
    spectra = shifted_spectra(queries, offsets)
    dest_group = routes[:, 0]
    slot_index = dest_group * capacity + block_ranks(dest_group)
    selector = (
        jnp.arange(mass_count * capacity, dtype=jnp.int32)[:, None] == slot_index[None, :]
    ).astype(jnp.bfloat16)
    packed = jnp.dot(selector, spectra, preferred_element_type=jnp.float32).astype(jnp.bfloat16)
    packed = packed.reshape(mass_count, capacity, packed.shape[-1])
    own_mass = lax.axis_index("mass")
    chunks = []
    for distance in range(mass_count):
        outgoing = jnp.take(packed, (own_mass + distance) % mass_count, axis=0)
        if distance:
            outgoing = lax.ppermute(
                outgoing,
                "mass",
                [(source, (source + distance) % mass_count) for source in range(mass_count)],
            )
        chunks.append(outgoing)
    arrived = jnp.concatenate(chunks, axis=0)
    part = arrived.shape[0] // 2
    part_a = ring_gather(ring_gather(arrived[:part], "x"), "z")
    part_b = ring_gather(ring_gather(arrived[part:], "z"), "x")
    own_side = jnp.concatenate(
        [part_a.reshape(-1, arrived.shape[1]), part_b.reshape(-1, arrived.shape[1])], axis=0
    )
    partner = [(core, core_count - 1 - core) for core in range(core_count)]
    other_side = lax.ppermute(own_side, "core", partner)
    own_best = column_topk(
        lax.dot_general(
            library, own_side, (((1,), (1,)), ((), ())), preferred_element_type=jnp.float32
        )
    )
    other_best = column_topk(
        lax.dot_general(
            library, other_side, (((1,), (1,)), ((), ())), preferred_element_type=jnp.float32
        )
    )
    local_best = jnp.concatenate([own_best, other_best], axis=1).T
    row = jnp.arange(local_best.shape[0], dtype=jnp.int32)
    slot = row % capacity
    source = row // capacity
    source_core = source % core_count
    source_z = source // core_count % z_count
    source_x = source // (core_count * z_count) % x_count
    source_mass = source // shard_count
    step_x = (source_x - lax.axis_index("x")) % x_count
    step_z = (source_z - lax.axis_index("z")) % z_count
    side = jnp.where(source_core == lax.axis_index("core"), 0, 1)
    in_part = (own_mass - source_mass) % mass_count * capacity + slot
    column_a = (step_z * x_count + step_x) * part + in_part
    column_b = (x_count * z_count + step_x * z_count + step_z) * part + in_part - part
    column = side * (shard_count // core_count) * 2 * part + jnp.where(in_part < part, column_a, column_b)
    outgoing = jnp.take(local_best, column, axis=0).reshape(-1, capacity, TOP_K)
    received = lax.all_to_all(
        outgoing, ("mass", "x", "z", "core"), split_axis=0, concat_axis=0, tiled=True
    )
    received = received.reshape(mass_count, shard_count, capacity, TOP_K)
    received = received.transpose(0, 2, 1, 3).reshape(mass_count * capacity, -1)
    candidates = jnp.take(received, slot_index, axis=0)
    return lax.top_k(candidates, TOP_K)[0]


def solution(mesh):
    mass_count, shard_count = mesh.devices.shape
    core_count = 2
    side = 4
    split_mesh = Mesh(
        mesh.devices.reshape(mass_count, side, shard_count // (side * core_count), core_count),
        ("mass", "x", "z", "core"),
    )
    spread = ("mass", "x", "z", "core")
    placed = (P(spread, None), P(spread, None), P(spread, None), P(spread))
    return jax.shard_map(
        per_device,
        mesh=split_mesh,
        in_specs=placed,
        out_specs=P(spread, None),
        check_vma=False,
    )
```

```python
import functools

import jax
import jax.numpy as jnp
from jax import lax
from jax.experimental import pallas as pl
from jax.experimental.pallas import tpu as pltpu
from jax.sharding import Mesh
from jax.sharding import PartitionSpec as P

MAX_SHIFT = 2048
TOP_K = 16
LANES = 128
SUBLANES = 8


def shifted_spectra(queries, offsets):
    row_count = queries.shape[0]
    bin_count = queries.shape[1]
    margin = jnp.zeros((row_count, MAX_SHIFT), queries.dtype)
    current = jnp.concatenate([margin, queries, margin], axis=1)
    window_start = MAX_SHIFT - offsets
    bit_total = (2 * MAX_SHIFT).bit_length()
    for bit_number in range(bit_total):
        step_size = 1 << bit_number
        moved = jnp.concatenate(
            [current[:, step_size:], jnp.zeros((row_count, step_size), current.dtype)], axis=1
        )
        taken = window_start >> bit_number & 1 == 1
        current = jnp.where(taken[:, None], moved, current)
    shifted = current[:, :bin_count]
    combined = queries.astype(jnp.float32) + shifted.astype(jnp.float32)
    scale_factor = lax.rsqrt(jnp.mean(combined * combined, axis=1, keepdims=True) + 1e-06)
    return (combined * scale_factor).astype(jnp.bfloat16)


def block_ranks(dest_group):
    length = dest_group.shape[0]
    position_ids = jnp.arange(length, dtype=jnp.int32)
    earlier = (dest_group[:, None] == dest_group[None, :]) & (
        position_ids[:, None] > position_ids[None, :]
    )
    return jnp.sum(earlier.astype(jnp.int32), axis=1)


def merge_sorted(first, second):
    merged = [jnp.maximum(first[k], second[TOP_K - 1 - k]) for k in range(TOP_K)]
    span = TOP_K // 2
    while span >= 1:
        for k in range(TOP_K):
            if (k // span) % 2 == 0:
                upper, lower = merged[k], merged[k + span]
                merged[k] = jnp.maximum(upper, lower)
                merged[k + span] = jnp.minimum(upper, lower)
        span //= 2
    return merged


def bitonic_sort(values):
    values = list(values)
    width = 2
    while width <= TOP_K:
        span = width // 2
        while span >= 1:
            for i in range(TOP_K):
                j = i ^ span
                if j > i:
                    high = jnp.maximum(values[i], values[j])
                    low = jnp.minimum(values[i], values[j])
                    if i & width == 0:
                        values[i], values[j] = high, low
                    else:
                        values[i], values[j] = low, high
            span //= 2
        width *= 2
    return values


def column_topk_kernel(scores_ref, out_ref):
    group = SUBLANES * TOP_K
    steps = scores_ref.shape[0] // group
    lowest = jnp.full((SUBLANES, LANES), -jnp.inf, jnp.float32)
    for column in range(0, scores_ref.shape[1], LANES):
        lanes = pl.ds(column, LANES)

        def insert(step, kept):
            start = pl.multiple_of(step * group, group)
            values = [
                scores_ref[pl.ds(start + SUBLANES * k, SUBLANES), lanes] for k in range(TOP_K)
            ]
            return tuple(merge_sorted(list(kept), bitonic_sort(values)))

        kept = lax.fori_loop(0, steps, insert, (lowest,) * TOP_K, unroll=2)
        kept = list(kept)
        shift = SUBLANES // 2
        while shift >= 1:
            rolled = [pltpu.roll(kept[k], shift, 0) for k in range(TOP_K)]
            kept = merge_sorted(kept, rolled)
            shift //= 2
        for k in range(TOP_K):
            out_ref[pl.ds(k, 1), lanes] = kept[k][0:1, :]


def column_topk(scores):
    rows, columns = scores.shape
    width = 2 * LANES if columns % (2 * LANES) == 0 else LANES
    return pl.pallas_call(
        column_topk_kernel,
        out_shape=jax.ShapeDtypeStruct((TOP_K, columns), jnp.float32),
        grid=(columns // width,),
        in_specs=[pl.BlockSpec((rows, width), lambda j: (0, j))],
        out_specs=pl.BlockSpec((TOP_K, width), lambda j: (0, j)),
        cost_estimate=pl.CostEstimate(
            flops=2 * TOP_K * rows * columns, transcendentals=0, bytes_accessed=4 * rows * columns
        ),
    )(scores)


def row_topk(values):
    count = values.shape[0]
    padded = jnp.pad(values.T, ((0, 0), (0, LANES - count)), constant_values=-jnp.inf)
    return column_topk(padded)[:, :count].T


def ring_gather(block, axis):
    size = 4
    flat = block.reshape(-1, block.shape[-1])
    half = flat.shape[0] // 2
    forward = [(i, (i + 1) % size) for i in range(size)]
    backward = [(i, (i - 1) % size) for i in range(size)]
    from_minus = lax.ppermute(flat, axis, forward)
    from_plus = lax.ppermute(flat, axis, backward)
    far_first = lax.ppermute(from_minus[:half], axis, forward)
    far_second = lax.ppermute(from_plus[half:], axis, backward)
    far = jnp.concatenate([far_first, far_second], axis=0)
    stacked = jnp.stack([flat, from_plus, far, from_minus])
    return stacked.reshape((size,) + block.shape)


def per_device(queries, library, routes, offsets):
    mass_count = lax.axis_size("mass")
    x_count = lax.axis_size("x")
    z_count = lax.axis_size("z")
    core_count = lax.axis_size("core")
    shard_count = x_count * z_count * core_count
    query_count = queries.shape[0]
    capacity = query_count // 2
    spectra = shifted_spectra(queries, offsets)
    dest_group = routes[:, 0]
    slot_index = dest_group * capacity + block_ranks(dest_group)
    selector = (
        jnp.arange(mass_count * capacity, dtype=jnp.int32)[:, None] == slot_index[None, :]
    ).astype(jnp.bfloat16)
    packed = jnp.dot(selector, spectra, preferred_element_type=jnp.float32).astype(jnp.bfloat16)
    packed = packed.reshape(mass_count, capacity, packed.shape[-1])
    own_mass = lax.axis_index("mass")
    chunks = []
    for distance in range(mass_count):
        outgoing = jnp.take(packed, (own_mass + distance) % mass_count, axis=0)
        if distance:
            outgoing = lax.ppermute(
                outgoing,
                "mass",
                [(source, (source + distance) % mass_count) for source in range(mass_count)],
            )
        chunks.append(outgoing)
    arrived = jnp.concatenate(chunks, axis=0)
    part = arrived.shape[0] // 2
    part_a = ring_gather(ring_gather(arrived[:part], "x"), "z")
    part_b = ring_gather(ring_gather(arrived[part:], "z"), "x")
    own_side = jnp.concatenate(
        [part_a.reshape(-1, arrived.shape[1]), part_b.reshape(-1, arrived.shape[1])], axis=0
    )
    partner = [(core, core_count - 1 - core) for core in range(core_count)]
    other_side = lax.ppermute(own_side, "core", partner)
    own_best = column_topk(
        lax.dot_general(
            library, own_side, (((1,), (1,)), ((), ())), preferred_element_type=jnp.float32
        )
    )
    other_best = column_topk(
        lax.dot_general(
            library, other_side, (((1,), (1,)), ((), ())), preferred_element_type=jnp.float32
        )
    )
    local_best = jnp.concatenate([own_best, other_best], axis=1).T
    row = jnp.arange(local_best.shape[0], dtype=jnp.int32)
    slot = row % capacity
    source = row // capacity
    source_core = source % core_count
    source_z = source // core_count % z_count
    source_x = source // (core_count * z_count) % x_count
    source_mass = source // shard_count
    step_x = (source_x - lax.axis_index("x")) % x_count
    step_z = (source_z - lax.axis_index("z")) % z_count
    side = jnp.where(source_core == lax.axis_index("core"), 0, 1)
    in_part = (own_mass - source_mass) % mass_count * capacity + slot
    column_a = (step_z * x_count + step_x) * part + in_part
    column_b = (x_count * z_count + step_x * z_count + step_z) * part + in_part - part
    column = side * (shard_count // core_count) * 2 * part + jnp.where(in_part < part, column_a, column_b)
    outgoing = jnp.take(local_best, column, axis=0).reshape(-1, capacity, TOP_K)
    received = lax.all_to_all(
        outgoing, ("mass", "x", "z", "core"), split_axis=0, concat_axis=0, tiled=True
    )
    received = received.reshape(mass_count, shard_count, capacity, TOP_K)
    received = received.transpose(0, 2, 1, 3).reshape(mass_count * capacity, -1)
    candidates = jnp.take(received, slot_index, axis=0)
    return row_topk(candidates)


def solution(mesh):
    mass_count, shard_count = mesh.devices.shape
    core_count = 2
    side = 4
    split_mesh = Mesh(
        mesh.devices.reshape(mass_count, side, shard_count // (side * core_count), core_count),
        ("mass", "x", "z", "core"),
    )
    spread = ("mass", "x", "z", "core")
    placed = (P(spread, None), P(spread, None), P(spread, None), P(spread))
    return jax.shard_map(
        per_device,
        mesh=split_mesh,
        in_specs=placed,
        out_specs=P(spread, None),
        check_vma=False,
    )
```

```python
import functools

import jax
import jax.numpy as jnp
from jax import lax
from jax.experimental import pallas as pl
from jax.experimental.pallas import tpu as pltpu
from jax.sharding import Mesh
from jax.sharding import PartitionSpec as P

MAX_SHIFT = 2048
TOP_K = 16
LANES = 128
SUBLANES = 8


def shifted_spectra(queries, offsets):
    row_count = queries.shape[0]
    bin_count = queries.shape[1]
    margin = jnp.zeros((row_count, MAX_SHIFT), queries.dtype)
    current = jnp.concatenate([margin, queries, margin], axis=1)
    window_start = MAX_SHIFT - offsets
    bit_total = (2 * MAX_SHIFT).bit_length()
    for bit_number in range(bit_total):
        step_size = 1 << bit_number
        moved = jnp.concatenate(
            [current[:, step_size:], jnp.zeros((row_count, step_size), current.dtype)], axis=1
        )
        taken = window_start >> bit_number & 1 == 1
        current = jnp.where(taken[:, None], moved, current)
    shifted = current[:, :bin_count]
    combined = queries.astype(jnp.float32) + shifted.astype(jnp.float32)
    scale_factor = lax.rsqrt(jnp.mean(combined * combined, axis=1, keepdims=True) + 1e-06)
    return (combined * scale_factor).astype(jnp.bfloat16)


def block_ranks(dest_group):
    length = dest_group.shape[0]
    position_ids = jnp.arange(length, dtype=jnp.int32)
    earlier = (dest_group[:, None] == dest_group[None, :]) & (
        position_ids[:, None] > position_ids[None, :]
    )
    return jnp.sum(earlier.astype(jnp.int32), axis=1)


def merge_sorted(first, second):
    merged = [jnp.maximum(first[k], second[TOP_K - 1 - k]) for k in range(TOP_K)]
    span = TOP_K // 2
    while span >= 1:
        for k in range(TOP_K):
            if (k // span) % 2 == 0:
                upper, lower = merged[k], merged[k + span]
                merged[k] = jnp.maximum(upper, lower)
                merged[k + span] = jnp.minimum(upper, lower)
        span //= 2
    return merged


def bitonic_sort(values):
    values = list(values)
    width = 2
    while width <= TOP_K:
        span = width // 2
        while span >= 1:
            for i in range(TOP_K):
                j = i ^ span
                if j > i:
                    high = jnp.maximum(values[i], values[j])
                    low = jnp.minimum(values[i], values[j])
                    if i & width == 0:
                        values[i], values[j] = high, low
                    else:
                        values[i], values[j] = low, high
            span //= 2
        width *= 2
    return values


def column_topk_kernel(scores_ref, out_ref):
    group = SUBLANES * TOP_K
    steps = scores_ref.shape[0] // group
    lowest = jnp.full((SUBLANES, LANES), -jnp.inf, jnp.float32)
    for column in range(0, scores_ref.shape[1], LANES):
        lanes = pl.ds(column, LANES)

        def insert(step, kept):
            start = pl.multiple_of(step * group, group)
            values = [
                scores_ref[pl.ds(start + SUBLANES * k, SUBLANES), lanes] for k in range(TOP_K)
            ]
            return tuple(merge_sorted(list(kept), bitonic_sort(values)))

        kept = lax.fori_loop(0, steps, insert, (lowest,) * TOP_K, unroll=2)
        kept = list(kept)
        shift = SUBLANES // 2
        while shift >= 1:
            rolled = [pltpu.roll(kept[k], shift, 0) for k in range(TOP_K)]
            kept = merge_sorted(kept, rolled)
            shift //= 2
        for k in range(TOP_K):
            out_ref[pl.ds(k, 1), lanes] = kept[k][0:1, :]


def column_topk(scores):
    rows, columns = scores.shape
    width = 2 * LANES if columns % (2 * LANES) == 0 else LANES
    return pl.pallas_call(
        column_topk_kernel,
        out_shape=jax.ShapeDtypeStruct((TOP_K, columns), jnp.float32),
        grid=(columns // width,),
        in_specs=[pl.BlockSpec((rows, width), lambda j: (0, j))],
        out_specs=pl.BlockSpec((TOP_K, width), lambda j: (0, j)),
        cost_estimate=pl.CostEstimate(
            flops=2 * TOP_K * rows * columns, transcendentals=0, bytes_accessed=4 * rows * columns
        ),
    )(scores)


def ring_gather(block, axis):
    size = 4
    flat = block.reshape(-1, block.shape[-1])
    half = flat.shape[0] // 2
    forward = [(i, (i + 1) % size) for i in range(size)]
    backward = [(i, (i - 1) % size) for i in range(size)]
    from_minus = lax.ppermute(flat, axis, forward)
    from_plus = lax.ppermute(flat, axis, backward)
    far_first = lax.ppermute(from_minus[:half], axis, forward)
    far_second = lax.ppermute(from_plus[half:], axis, backward)
    far = jnp.concatenate([far_first, far_second], axis=0)
    stacked = jnp.stack([flat, from_plus, far, from_minus])
    return stacked.reshape((size,) + block.shape)


def per_device(queries, library, routes, offsets):
    mass_count = lax.axis_size("mass")
    x_count = lax.axis_size("x")
    z_count = lax.axis_size("z")
    core_count = lax.axis_size("core")
    shard_count = x_count * z_count * core_count
    query_count = queries.shape[0]
    capacity = query_count // 2
    spectra = shifted_spectra(queries, offsets)
    dest_group = routes[:, 0]
    slot_index = dest_group * capacity + block_ranks(dest_group)
    selector = (
        jnp.arange(mass_count * capacity, dtype=jnp.int32)[:, None] == slot_index[None, :]
    ).astype(jnp.bfloat16)
    packed = jnp.dot(selector, spectra, preferred_element_type=jnp.float32).astype(jnp.bfloat16)
    packed = packed.reshape(mass_count, capacity, packed.shape[-1])
    own_mass = lax.axis_index("mass")
    chunks = []
    for distance in range(mass_count):
        outgoing = jnp.take(packed, (own_mass + distance) % mass_count, axis=0)
        if distance:
            outgoing = lax.ppermute(
                outgoing,
                "mass",
                [(source, (source + distance) % mass_count) for source in range(mass_count)],
            )
        chunks.append(outgoing)
    arrived = jnp.concatenate(chunks, axis=0)
    part = arrived.shape[0] // 2
    part_a = ring_gather(ring_gather(arrived[:part], "x"), "z")
    part_b = ring_gather(ring_gather(arrived[part:], "z"), "x")
    own_side = jnp.concatenate(
        [part_a.reshape(-1, arrived.shape[1]), part_b.reshape(-1, arrived.shape[1])], axis=0
    )
    partner = [(core, core_count - 1 - core) for core in range(core_count)]
    other_side = lax.ppermute(own_side, "core", partner)
    own_best = column_topk(
        lax.dot_general(
            library, own_side, (((1,), (1,)), ((), ())), preferred_element_type=jnp.float32
        )
    )
    other_best = column_topk(
        lax.dot_general(
            library, other_side, (((1,), (1,)), ((), ())), preferred_element_type=jnp.float32
        )
    )
    local_best = jnp.concatenate([own_best, other_best], axis=1).T
    row = jnp.arange(local_best.shape[0], dtype=jnp.int32)
    slot = row % capacity
    source = row // capacity
    source_core = source % core_count
    source_z = source // core_count % z_count
    source_x = source // (core_count * z_count) % x_count
    source_mass = source // shard_count
    step_x = (source_x - lax.axis_index("x")) % x_count
    step_z = (source_z - lax.axis_index("z")) % z_count
    side = jnp.where(source_core == lax.axis_index("core"), 0, 1)
    in_part = (own_mass - source_mass) % mass_count * capacity + slot
    column_a = (step_z * x_count + step_x) * part + in_part
    column_b = (x_count * z_count + step_x * z_count + step_z) * part + in_part - part
    column = side * (shard_count // core_count) * 2 * part + jnp.where(in_part < part, column_a, column_b)
    outgoing = jnp.take(local_best, column, axis=0).reshape(-1, capacity, TOP_K)
    received = lax.all_to_all(
        outgoing, ("mass", "x", "z", "core"), split_axis=0, concat_axis=0, tiled=True
    )
    received = received.reshape(mass_count, shard_count, capacity, TOP_K)
    received = received.transpose(0, 2, 1, 3).reshape(mass_count * capacity, -1)
    candidates = jnp.take(received, slot_index, axis=0)
    return lax.top_k(candidates, TOP_K)[0]


def solution(mesh):
    mass_count, shard_count = mesh.devices.shape
    core_count = 2
    side = 4
    split_mesh = Mesh(
        mesh.devices.reshape(mass_count, side, shard_count // (side * core_count), core_count),
        ("mass", "x", "z", "core"),
    )
    spread = ("mass", "x", "z", "core")
    placed = (P(spread, None), P(spread, None), P(spread, None), P(spread))
    return jax.shard_map(
        per_device,
        mesh=split_mesh,
        in_specs=placed,
        out_specs=P(spread, None),
        check_vma=False,
    )
```

```python
import functools

import jax
import jax.numpy as jnp
from jax import lax
from jax.experimental import pallas as pl
from jax.experimental.pallas import tpu as pltpu
from jax.sharding import Mesh
from jax.sharding import PartitionSpec as P

MAX_SHIFT = 2048
TOP_K = 16
LANES = 128
SUBLANES = 8


def shifted_spectra(queries, offsets):
    row_count = queries.shape[0]
    bin_count = queries.shape[1]
    margin = jnp.zeros((row_count, MAX_SHIFT), queries.dtype)
    current = jnp.concatenate([margin, queries, margin], axis=1)
    window_start = MAX_SHIFT - offsets
    bit_total = (2 * MAX_SHIFT).bit_length()
    for bit_number in range(bit_total):
        step_size = 1 << bit_number
        moved = jnp.concatenate(
            [current[:, step_size:], jnp.zeros((row_count, step_size), current.dtype)], axis=1
        )
        taken = window_start >> bit_number & 1 == 1
        current = jnp.where(taken[:, None], moved, current)
    shifted = current[:, :bin_count]
    combined = queries.astype(jnp.float32) + shifted.astype(jnp.float32)
    scale_factor = lax.rsqrt(jnp.mean(combined * combined, axis=1, keepdims=True) + 1e-06)
    return (combined * scale_factor).astype(jnp.bfloat16)


def block_ranks(dest_group):
    length = dest_group.shape[0]
    position_ids = jnp.arange(length, dtype=jnp.int32)
    earlier = (dest_group[:, None] == dest_group[None, :]) & (
        position_ids[:, None] > position_ids[None, :]
    )
    return jnp.sum(earlier.astype(jnp.int32), axis=1)


def merge_sorted(first, second):
    merged = [jnp.maximum(first[k], second[TOP_K - 1 - k]) for k in range(TOP_K)]
    span = TOP_K // 2
    while span >= 1:
        for k in range(TOP_K):
            if (k // span) % 2 == 0:
                upper, lower = merged[k], merged[k + span]
                merged[k] = jnp.maximum(upper, lower)
                merged[k + span] = jnp.minimum(upper, lower)
        span //= 2
    return merged


def bitonic_sort(values):
    values = list(values)
    width = 2
    while width <= TOP_K:
        span = width // 2
        while span >= 1:
            for i in range(TOP_K):
                j = i ^ span
                if j > i:
                    high = jnp.maximum(values[i], values[j])
                    low = jnp.minimum(values[i], values[j])
                    if i & width == 0:
                        values[i], values[j] = high, low
                    else:
                        values[i], values[j] = low, high
            span //= 2
        width *= 2
    return values


def column_topk_kernel(scores_ref, out_ref):
    group = SUBLANES * TOP_K
    steps = scores_ref.shape[0] // group
    lowest = jnp.full((SUBLANES, LANES), -jnp.inf, jnp.float32)
    for column in range(0, scores_ref.shape[1], LANES):
        lanes = pl.ds(column, LANES)

        def insert(step, kept):
            start = pl.multiple_of(step * group, group)
            values = [
                scores_ref[pl.ds(start + SUBLANES * k, SUBLANES), lanes] for k in range(TOP_K)
            ]
            return tuple(merge_sorted(list(kept), bitonic_sort(values)))

        kept = lax.fori_loop(0, steps, insert, (lowest,) * TOP_K, unroll=True)
        kept = list(kept)
        shift = SUBLANES // 2
        while shift >= 1:
            rolled = [pltpu.roll(kept[k], shift, 0) for k in range(TOP_K)]
            kept = merge_sorted(kept, rolled)
            shift //= 2
        for k in range(TOP_K):
            out_ref[pl.ds(k, 1), lanes] = kept[k][0:1, :]


def column_topk(scores):
    rows, columns = scores.shape
    width = 2 * LANES if columns % (2 * LANES) == 0 else LANES
    return pl.pallas_call(
        column_topk_kernel,
        out_shape=jax.ShapeDtypeStruct((TOP_K, columns), jnp.float32),
        grid=(columns // width,),
        in_specs=[pl.BlockSpec((rows, width), lambda j: (0, j))],
        out_specs=pl.BlockSpec((TOP_K, width), lambda j: (0, j)),
        cost_estimate=pl.CostEstimate(
            flops=2 * TOP_K * rows * columns, transcendentals=0, bytes_accessed=4 * rows * columns
        ),
    )(scores)


def ring_gather(block, axis):
    size = 4
    flat = block.reshape(-1, block.shape[-1])
    half = flat.shape[0] // 2
    forward = [(i, (i + 1) % size) for i in range(size)]
    backward = [(i, (i - 1) % size) for i in range(size)]
    from_minus = lax.ppermute(flat, axis, forward)
    from_plus = lax.ppermute(flat, axis, backward)
    far_first = lax.ppermute(from_minus[:half], axis, forward)
    far_second = lax.ppermute(from_plus[half:], axis, backward)
    far = jnp.concatenate([far_first, far_second], axis=0)
    stacked = jnp.stack([flat, from_plus, far, from_minus])
    return stacked.reshape((size,) + block.shape)


def per_device(queries, library, routes, offsets):
    mass_count = lax.axis_size("mass")
    x_count = lax.axis_size("x")
    z_count = lax.axis_size("z")
    core_count = lax.axis_size("core")
    shard_count = x_count * z_count * core_count
    query_count = queries.shape[0]
    capacity = query_count // 2
    spectra = shifted_spectra(queries, offsets)
    dest_group = routes[:, 0]
    slot_index = dest_group * capacity + block_ranks(dest_group)
    selector = (
        jnp.arange(mass_count * capacity, dtype=jnp.int32)[:, None] == slot_index[None, :]
    ).astype(jnp.bfloat16)
    packed = jnp.dot(selector, spectra, preferred_element_type=jnp.float32).astype(jnp.bfloat16)
    packed = packed.reshape(mass_count, capacity, packed.shape[-1])
    own_mass = lax.axis_index("mass")
    chunks = []
    for distance in range(mass_count):
        outgoing = jnp.take(packed, (own_mass + distance) % mass_count, axis=0)
        if distance:
            outgoing = lax.ppermute(
                outgoing,
                "mass",
                [(source, (source + distance) % mass_count) for source in range(mass_count)],
            )
        chunks.append(outgoing)
    arrived = jnp.concatenate(chunks, axis=0)
    part = arrived.shape[0] // 2
    part_a = ring_gather(ring_gather(arrived[:part], "x"), "z")
    part_b = ring_gather(ring_gather(arrived[part:], "z"), "x")
    own_side = jnp.concatenate(
        [part_a.reshape(-1, arrived.shape[1]), part_b.reshape(-1, arrived.shape[1])], axis=0
    )
    partner = [(core, core_count - 1 - core) for core in range(core_count)]
    other_side = lax.ppermute(own_side, "core", partner)
    own_best = column_topk(
        lax.dot_general(
            library, own_side, (((1,), (1,)), ((), ())), preferred_element_type=jnp.float32
        )
    )
    other_best = column_topk(
        lax.dot_general(
            library, other_side, (((1,), (1,)), ((), ())), preferred_element_type=jnp.float32
        )
    )
    local_best = jnp.concatenate([own_best, other_best], axis=1).T
    row = jnp.arange(local_best.shape[0], dtype=jnp.int32)
    slot = row % capacity
    source = row // capacity
    source_core = source % core_count
    source_z = source // core_count % z_count
    source_x = source // (core_count * z_count) % x_count
    source_mass = source // shard_count
    step_x = (source_x - lax.axis_index("x")) % x_count
    step_z = (source_z - lax.axis_index("z")) % z_count
    side = jnp.where(source_core == lax.axis_index("core"), 0, 1)
    in_part = (own_mass - source_mass) % mass_count * capacity + slot
    column_a = (step_z * x_count + step_x) * part + in_part
    column_b = (x_count * z_count + step_x * z_count + step_z) * part + in_part - part
    column = side * (shard_count // core_count) * 2 * part + jnp.where(in_part < part, column_a, column_b)
    outgoing = jnp.take(local_best, column, axis=0).reshape(-1, capacity, TOP_K)
    received = lax.all_to_all(
        outgoing, ("mass", "x", "z", "core"), split_axis=0, concat_axis=0, tiled=True
    )
    received = received.reshape(mass_count, shard_count, capacity, TOP_K)
    received = received.transpose(0, 2, 1, 3).reshape(mass_count * capacity, -1)
    candidates = jnp.take(received, slot_index, axis=0)
    return lax.top_k(candidates, TOP_K)[0]


def solution(mesh):
    mass_count, shard_count = mesh.devices.shape
    core_count = 2
    side = 4
    split_mesh = Mesh(
        mesh.devices.reshape(mass_count, side, shard_count // (side * core_count), core_count),
        ("mass", "x", "z", "core"),
    )
    spread = ("mass", "x", "z", "core")
    placed = (P(spread, None), P(spread, None), P(spread, None), P(spread))
    return jax.shard_map(
        per_device,
        mesh=split_mesh,
        in_specs=placed,
        out_specs=P(spread, None),
        check_vma=False,
    )
```

```python
import functools

import jax
import jax.numpy as jnp
from jax import lax
from jax.experimental import pallas as pl
from jax.experimental.pallas import tpu as pltpu
from jax.sharding import Mesh
from jax.sharding import PartitionSpec as P

MAX_SHIFT = 2048
TOP_K = 16
LANES = 128
SUBLANES = 8


def shifted_spectra(queries, offsets):
    row_count = queries.shape[0]
    bin_count = queries.shape[1]
    margin = jnp.zeros((row_count, MAX_SHIFT), queries.dtype)
    current = jnp.concatenate([margin, queries, margin], axis=1)
    window_start = MAX_SHIFT - offsets
    bit_total = (2 * MAX_SHIFT).bit_length()
    for bit_number in range(bit_total):
        step_size = 1 << bit_number
        moved = jnp.concatenate(
            [current[:, step_size:], jnp.zeros((row_count, step_size), current.dtype)], axis=1
        )
        taken = window_start >> bit_number & 1 == 1
        current = jnp.where(taken[:, None], moved, current)
    shifted = current[:, :bin_count]
    combined = queries.astype(jnp.float32) + shifted.astype(jnp.float32)
    scale_factor = lax.rsqrt(jnp.mean(combined * combined, axis=1, keepdims=True) + 1e-06)
    return (combined * scale_factor).astype(jnp.bfloat16)


def block_ranks(dest_group):
    length = dest_group.shape[0]
    position_ids = jnp.arange(length, dtype=jnp.int32)
    earlier = (dest_group[:, None] == dest_group[None, :]) & (
        position_ids[:, None] > position_ids[None, :]
    )
    return jnp.sum(earlier.astype(jnp.int32), axis=1)


def merge_sorted(first, second):
    merged = [jnp.maximum(first[k], second[TOP_K - 1 - k]) for k in range(TOP_K)]
    span = TOP_K // 2
    while span >= 1:
        for k in range(TOP_K):
            if (k // span) % 2 == 0:
                upper, lower = merged[k], merged[k + span]
                merged[k] = jnp.maximum(upper, lower)
                merged[k + span] = jnp.minimum(upper, lower)
        span //= 2
    return merged


def bitonic_sort(values):
    values = list(values)
    width = 2
    while width <= TOP_K:
        span = width // 2
        while span >= 1:
            for i in range(TOP_K):
                j = i ^ span
                if j > i:
                    high = jnp.maximum(values[i], values[j])
                    low = jnp.minimum(values[i], values[j])
                    if i & width == 0:
                        values[i], values[j] = high, low
                    else:
                        values[i], values[j] = low, high
            span //= 2
        width *= 2
    return values


def column_topk_kernel(scores_ref, out_ref):
    group = SUBLANES * TOP_K
    steps = scores_ref.shape[0] // group
    lowest = jnp.full((SUBLANES, LANES), -jnp.inf, jnp.float32)
    for column in range(0, scores_ref.shape[1], LANES):
        lanes = pl.ds(column, LANES)

        def insert(step, kept):
            start = pl.multiple_of(step * group, group)
            values = [
                scores_ref[pl.ds(start + SUBLANES * k, SUBLANES), lanes] for k in range(TOP_K)
            ]
            return tuple(merge_sorted(list(kept), bitonic_sort(values)))

        kept = lax.fori_loop(0, steps, insert, (lowest,) * TOP_K, unroll=True)
        kept = list(kept)
        shift = SUBLANES // 2
        while shift >= 1:
            rolled = [pltpu.roll(kept[k], shift, 0) for k in range(TOP_K)]
            kept = merge_sorted(kept, rolled)
            shift //= 2
        for k in range(TOP_K):
            out_ref[pl.ds(k, 1), lanes] = kept[k][0:1, :]


def column_topk(scores):
    rows, columns = scores.shape
    width = 4 * LANES if columns % (4 * LANES) == 0 else LANES
    return pl.pallas_call(
        column_topk_kernel,
        out_shape=jax.ShapeDtypeStruct((TOP_K, columns), jnp.float32),
        grid=(columns // width,),
        in_specs=[pl.BlockSpec((rows, width), lambda j: (0, j))],
        out_specs=pl.BlockSpec((TOP_K, width), lambda j: (0, j)),
        cost_estimate=pl.CostEstimate(
            flops=2 * TOP_K * rows * columns, transcendentals=0, bytes_accessed=4 * rows * columns
        ),
    )(scores)


def ring_gather(block, axis):
    size = 4
    flat = block.reshape(-1, block.shape[-1])
    half = flat.shape[0] // 2
    forward = [(i, (i + 1) % size) for i in range(size)]
    backward = [(i, (i - 1) % size) for i in range(size)]
    from_minus = lax.ppermute(flat, axis, forward)
    from_plus = lax.ppermute(flat, axis, backward)
    far_first = lax.ppermute(from_minus[:half], axis, forward)
    far_second = lax.ppermute(from_plus[half:], axis, backward)
    far = jnp.concatenate([far_first, far_second], axis=0)
    stacked = jnp.stack([flat, from_plus, far, from_minus])
    return stacked.reshape((size,) + block.shape)


def per_device(queries, library, routes, offsets):
    mass_count = lax.axis_size("mass")
    x_count = lax.axis_size("x")
    z_count = lax.axis_size("z")
    core_count = lax.axis_size("core")
    shard_count = x_count * z_count * core_count
    query_count = queries.shape[0]
    capacity = query_count // 2
    spectra = shifted_spectra(queries, offsets)
    dest_group = routes[:, 0]
    slot_index = dest_group * capacity + block_ranks(dest_group)
    selector = (
        jnp.arange(mass_count * capacity, dtype=jnp.int32)[:, None] == slot_index[None, :]
    ).astype(jnp.bfloat16)
    packed = jnp.dot(selector, spectra, preferred_element_type=jnp.float32).astype(jnp.bfloat16)
    packed = packed.reshape(mass_count, capacity, packed.shape[-1])
    own_mass = lax.axis_index("mass")
    chunks = []
    for distance in range(mass_count):
        outgoing = jnp.take(packed, (own_mass + distance) % mass_count, axis=0)
        if distance:
            outgoing = lax.ppermute(
                outgoing,
                "mass",
                [(source, (source + distance) % mass_count) for source in range(mass_count)],
            )
        chunks.append(outgoing)
    arrived = jnp.concatenate(chunks, axis=0)
    part = arrived.shape[0] // 2
    part_a = ring_gather(ring_gather(arrived[:part], "x"), "z")
    part_b = ring_gather(ring_gather(arrived[part:], "z"), "x")
    own_side = jnp.concatenate(
        [part_a.reshape(-1, arrived.shape[1]), part_b.reshape(-1, arrived.shape[1])], axis=0
    )
    partner = [(core, core_count - 1 - core) for core in range(core_count)]
    other_side = lax.ppermute(own_side, "core", partner)
    own_best = column_topk(
        lax.dot_general(
            library, own_side, (((1,), (1,)), ((), ())), preferred_element_type=jnp.float32
        )
    )
    other_best = column_topk(
        lax.dot_general(
            library, other_side, (((1,), (1,)), ((), ())), preferred_element_type=jnp.float32
        )
    )
    local_best = jnp.concatenate([own_best, other_best], axis=1).T
    row = jnp.arange(local_best.shape[0], dtype=jnp.int32)
    slot = row % capacity
    source = row // capacity
    source_core = source % core_count
    source_z = source // core_count % z_count
    source_x = source // (core_count * z_count) % x_count
    source_mass = source // shard_count
    step_x = (source_x - lax.axis_index("x")) % x_count
    step_z = (source_z - lax.axis_index("z")) % z_count
    side = jnp.where(source_core == lax.axis_index("core"), 0, 1)
    in_part = (own_mass - source_mass) % mass_count * capacity + slot
    column_a = (step_z * x_count + step_x) * part + in_part
    column_b = (x_count * z_count + step_x * z_count + step_z) * part + in_part - part
    column = side * (shard_count // core_count) * 2 * part + jnp.where(in_part < part, column_a, column_b)
    outgoing = jnp.take(local_best, column, axis=0).reshape(-1, capacity, TOP_K)
    received = lax.all_to_all(
        outgoing, ("mass", "x", "z", "core"), split_axis=0, concat_axis=0, tiled=True
    )
    received = received.reshape(mass_count, shard_count, capacity, TOP_K)
    received = received.transpose(0, 2, 1, 3).reshape(mass_count * capacity, -1)
    candidates = jnp.take(received, slot_index, axis=0)
    return lax.top_k(candidates, TOP_K)[0]


def solution(mesh):
    mass_count, shard_count = mesh.devices.shape
    core_count = 2
    side = 4
    split_mesh = Mesh(
        mesh.devices.reshape(mass_count, side, shard_count // (side * core_count), core_count),
        ("mass", "x", "z", "core"),
    )
    spread = ("mass", "x", "z", "core")
    placed = (P(spread, None), P(spread, None), P(spread, None), P(spread))
    return jax.shard_map(
        per_device,
        mesh=split_mesh,
        in_specs=placed,
        out_specs=P(spread, None),
        check_vma=False,
    )
```
